256 devices in a mesh: rep: 8 (over y_hi, x), ep: 32 (over z, y_lo, core).
Axes of the slice: x: 4, y: 4 (y_hi: 2, y_lo: 2; y = y_hi * 2 + y_lo), z: 8, core: 2. Of those that a mesh axis runs over, the one named last changes fastest.
Arguments:
- queries: bfloat16 [8, 128, 36864], P('rep', None, 'ep'), may hold values from -64 to 64
- suffix_latent: bfloat16 [8, 73728], P('rep', 'ep'), may hold values from -4 to 4
- cache_pool: bfloat16 [8, 256, 36864], P('rep', 'ep'), may hold values from -4 to 4
- holders: int32 [8, 64], replicated, may hold values from 0 to 7, as said below
- block_slots: int32 [8, 64], replicated, may hold values from 0 to 7, as said below
- prefix_len: int32 [8], P('rep'), may hold values from 1024 to 4096, as said below
- hidden: bfloat16 [8, 128, 7168], P('rep', 'ep'), may hold values from -16 to 16
- w_value: bfloat16 [64, 512, 128], P('ep'), may hold values from -0.25 to 0.25
- w_out: bfloat16 [8192, 7168], P('ep'), may hold values from -0.0625 to 0.0625
- norm_gain: bfloat16 [7168], replicated, may hold values from 0.099609375 to 1.8984375
- experts: int32 [8, 128, 8], P('rep', 'ep'), may hold values from 0 to 31, all different within a row; in each aligned block of 4 rows (0 to 3, 4 to 7, ..., all dimensions but the last counted through in order) at most 2 rows name the same one
- gate_weights: bfloat16 [8, 128, 8], P('rep', 'ep'), may hold values from 0.029907227 to 0.29882812
- w_gate: bfloat16 [32, 7168, 1024], P('ep', None, 'rep'), may hold values from -0.0625 to 0.0625
- w_up: bfloat16 [32, 7168, 1024], P('ep', None, 'rep'), may hold values from -0.0625 to 0.0625
- w_down: bfloat16 [32, 1024, 7168], P('ep', 'rep'), may hold values from -0.1875 to 0.1875
Outputs:
- layer_out: float32 [8, 128, 7168], P('rep', 'ep')
The draws below stay inside these ranges and needn't reach their ends.
Inputs may be any that keep to these rules, and one draw needn't show every extreme that they name: `holders`: for each group and each index s of ep, the blocks s * 2 to (s + 1) * 2 - 1 of its prefix come from holder groups none of which gives more than 1 of them. `block_slots`: block b of a prefix lies on index b // 2 of ep of its holder group. `prefix_len`: some group's prefix has 4096 tokens. Each row names 8 different experts; among the rows of one device no expert is named more than 2 times.
All inputs are finite; a program needn't handle non-finite values.
Results may differ from the reference program's by a relative error of at most 0.004.
Values may be sent and summed in bfloat16 or wider, within the bound.
No kernel may reach another device: no remote copies, remote signals or barrier semaphores. Data moves between devices by JAX's collectives and lax.ppermute only.
A program may use at most 128 MiB of HBM per device.

```python
import math
import jax
import jax.numpy as jnp
import numpy as np
from jax import lax

D = 7168
KVR = 512
VDIM = 128
TOP = 8
HEADS = 64
FF = 1024
BLK = 64
SUF = 128
PB_DEV = 2
POOL = 8
GROUPS = 8
LAT = 576
TOK_DEV = 4
EXPERTS = 32
CAP = 2
PBLK = 64
PMAX = 4096
POOL_REP = 256
FF_DEV = 128
N_REP = 8
N_EP = 32


def table_draw(key):
    device_count = PBLK // PB_DEV
    order_key = jax.random.fold_in(key, 11)
    ranking = jax.random.randint(order_key, (GROUPS, device_count, GROUPS), 0, 1 << 20)
    ranking = ranking * GROUPS + jnp.arange(GROUPS, dtype=jnp.int32)[None, None, :]
    ordering = jnp.argsort(ranking, axis=2, stable=True).astype(jnp.int32)
    cycling = jnp.arange(PB_DEV, dtype=jnp.int32) % GROUPS
    cycling = jnp.broadcast_to(cycling[None, None, :], (GROUPS, device_count, PB_DEV))
    holder_ids = jnp.take_along_axis(ordering, cycling, axis=2)
    slot_key = jax.random.fold_in(key, 12)
    slot_ids = jax.random.randint(slot_key, (GROUPS, device_count, PB_DEV), 0, POOL)
    return (holder_ids.reshape(GROUPS, PBLK).astype(jnp.int32), slot_ids.reshape(GROUPS, PBLK).astype(jnp.int32))


def length_draw(key):
    drawn = jax.random.randint(jax.random.fold_in(key, 13), (GROUPS,), PMAX // 4, PMAX + 1)
    longest = jax.random.randint(jax.random.fold_in(key, 14), (), 0, GROUPS)
    return jnp.where(jnp.arange(GROUPS) == longest, PMAX, drawn).astype(jnp.int32)


def pool_draw(key):
    pool_key = jax.random.fold_in(key, 15)
    drawn = jnp.clip(jax.random.normal(pool_key, (GROUPS, POOL_REP, BLK * LAT), jnp.float32), -4.0, 4.0)
    return drawn


def draw_cache_pool(key, part):
    return pool_draw(key).astype(jnp.bfloat16)


def draw_holders(key, part):
    return table_draw(key)[0]


def draw_block_slots(key, part):
    return table_draw(key)[1]


def draw_prefix_len(key, part):
    return length_draw(key)


def draw_queries(key, part):
    spread = 34.64 / math.sqrt(LAT)
    query_key = jax.random.fold_in(key, 16)
    drawn = jnp.clip(jax.random.normal(query_key, (GROUPS, SUF, HEADS, LAT), jnp.float32), -6.0, 6.0) * spread
    return drawn.reshape(GROUPS, SUF, HEADS * LAT).astype(jnp.bfloat16)


def draw_hidden(key, part):
    split_keys = jax.random.split(jax.random.fold_in(key, 19), 3)
    row_scale = jnp.exp(jax.random.uniform(split_keys[0], (GROUPS, SUF, 1), jnp.float32, math.log(0.15), math.log(1.5)))
    column_scale = jnp.exp(jax.random.uniform(split_keys[1], (1, 1, D), jnp.float32, math.log(0.15), math.log(1.5)))
    noise = jnp.clip(jax.random.normal(split_keys[2], (GROUPS, SUF, D), jnp.float32), -5.0, 5.0)
    drawn = row_scale * column_scale * noise
    return drawn.astype(jnp.bfloat16)


def levels(key, shape, shards, least, top_value):
    loudness, own = 1.0, jax.random.fold_in(key, 6)
    for dim, parts in shards:
        draws = jnp.exp(jax.random.uniform(jax.random.fold_in(own, dim), (parts,), jnp.float32, least / len(shards), top_value / len(shards)))
        loudness = loudness * jnp.repeat(draws, shape[dim] // parts).reshape([-1 if axis == dim else 1 for axis in range(len(shape))])
    return loudness


def routed_block(rng, own, number, rows, number_of, top, bound, lean):
    order = jax.random.permutation(rng, number_of)
    heavy_load, common = shares(number_of, rows * top, bound, lean, True), shares(number_of, rows * top, bound, lean, False)
    places = jnp.arange(number_of)

    def named(sizes, rotation):
        used = int((sizes > 0).sum())
        fixed = max(1, used // 4)
        shifted = fixed + (places - fixed + rotation * (used - fixed)) % max(1, number_of - fixed)
        return jnp.zeros((number_of,), jnp.int32).at[order[jnp.where(places < fixed, places, shifted)]].set(jnp.asarray(sizes, jnp.int32))

    sizes = jnp.where(number % 4 == 0, named(heavy_load, number // 4), named(common, number - number // 4 - 1))
    mixed = jax.random.permutation(jax.random.fold_in(own, 3), number_of)
    source_of, receiver = mixed[0:number_of // 2 * 2:2], mixed[1:number_of // 2 * 2:2]
    margin = jnp.minimum(sizes[source_of] - 1, bound - sizes[receiver]) // 2
    margin = jnp.where((source_of == order[0]) | (receiver == order[0]) | (sizes[receiver] == 0), 0, jnp.maximum(margin, 0))
    shifted = jax.random.randint(jax.random.fold_in(own, 4), (number_of // 2,), 0, 1 << 20) % (margin + 1)
    sizes = sizes.at[source_of].add(-shifted).at[receiver].add(shifted)
    items = jnp.searchsorted(jnp.cumsum(sizes), jnp.arange(rows * top), side="right").astype(jnp.int32)
    listing = items.reshape(top, rows).T
    listing = listing[jax.random.permutation(jax.random.fold_in(own, 1), rows)]
    rotation = jax.random.randint(jax.random.fold_in(own, 2), (rows, 1), 0, top)
    return jnp.take_along_axis(listing, (jnp.arange(top)[None, :] + rotation) % top, axis=1)


def shares(amount, total, bound, lean, full):
    weights = [(1 << 20) // math.isqrt(standing ** lean) + 1 for standing in range(1, amount + 1)]
    largest = bound if full else min(bound, max(-(-total // amount), total * weights[0] // sum(weights)))
    least = 1 if total - largest >= amount - 1 else 0
    given, surplus = [largest] + [least] * (amount - 1), total - largest - least * (amount - 1)
    while surplus > 0:
        free = [i for i in range(1, amount) if given[i] < largest] or [i for i in range(1, amount) if given[i] < bound]
        whole, remaining = sum([weights[i] for i in free]), surplus
        for i in free:
            more = min(bound - given[i], max(1, remaining * weights[i] // whole), surplus)
            given[i] = given[i] + more
            surplus = surplus - more
    return np.array(given)


def scatter_about(own_key, extent, deviation, most, cuts=(), held_as=jnp.bfloat16):
    values = jax.random.normal(own_key, extent, jnp.float32) * deviation
    if len(cuts) > 0:
        values = levels(own_key, extent, cuts, -0.22, 0.18) * values
    return jnp.clip(values, min=-most, max=most).astype(held_as)


def setup_inputs(seed: int = 0) -> dict:
    seeds = jax.random.split(jax.random.key(seed), 16)
    queries = draw_queries(jax.random.fold_in(seeds[15], 71), 0)
    suffix_latent = scatter_about(seeds[1], (GROUPS, SUF * LAT), 1.0, 4.0, ((0, 8), (1, 32)))
    cache_pool = draw_cache_pool(jax.random.fold_in(seeds[15], 71), 0)
    holders = draw_holders(jax.random.fold_in(seeds[15], 71), 0)
    block_slots = draw_block_slots(jax.random.fold_in(seeds[15], 71), 0)
    prefix_len = draw_prefix_len(jax.random.fold_in(seeds[15], 71), 0)
    hidden = draw_hidden(jax.random.fold_in(seeds[15], 71), 0)
    w_value = scatter_about(seeds[7], (HEADS, KVR, VDIM), KVR ** -0.5, 0.25, ((0, 32),))
    w_out = scatter_about(seeds[8], (HEADS * VDIM, D), (HEADS * VDIM) ** -0.5, 0.0625, ((0, 32),))
    norm_gain = jnp.clip(1.0 + 0.18 * jax.random.normal(seeds[9], (D,), jnp.float32), 0.099609375, 1.8984375).astype(jnp.bfloat16)
    experts_keys = jax.random.split(jax.random.fold_in(seeds[10], 1), GROUPS * SUF // TOK_DEV)
    experts_turns = jax.random.permutation(jax.random.fold_in(seeds[10], 3), GROUPS * SUF // TOK_DEV)
    experts = jax.vmap(lambda own, number: routed_block(jax.random.fold_in(seeds[10], 2), own, number, TOK_DEV, EXPERTS, TOP, CAP, 2))(experts_keys, experts_turns).reshape((GROUPS, SUF, TOP))
    gate_weights = jnp.clip(jnp.exp(math.log(0.29882812) - 2.30176843 * jax.random.uniform(seeds[11], (GROUPS, SUF, TOP), jnp.float32) ** levels(seeds[11], (GROUPS, SUF, TOP), ((0, 8), (1, 32)), -0.2, 0.2)), 0.029907227, 0.29882812).astype(jnp.bfloat16)
    w_gate = scatter_about(seeds[12], (EXPERTS, D, FF), D ** -0.5, 0.0625, ((0, 32), (2, 8)))
    w_up = scatter_about(seeds[13], (EXPERTS, D, FF), D ** -0.5, 0.0625, ((0, 32), (2, 8)))
    w_down = scatter_about(seeds[14], (EXPERTS, FF, D), FF ** -0.5, 0.1875, ((0, 32), (1, 8)))
    return {"queries": queries, "suffix_latent": suffix_latent, "cache_pool": cache_pool, "holders": holders, "block_slots": block_slots, "prefix_len": prefix_len, "hidden": hidden, "w_value": w_value, "w_out": w_out, "norm_gain": norm_gain, "experts": experts, "gate_weights": gate_weights, "w_gate": w_gate, "w_up": w_up, "w_down": w_down}


score_scale = 0.07216878364870323
norm_eps = 1e-06

def rounded(values):
    return lax.optimization_barrier(values.astype(jnp.bfloat16)).astype(jnp.float32)

def group_attention(query_group, suffix_group, holder_row, slot_row, length, cache_pool, w_value, w_out):
    blocks = jnp.arange(PBLK, dtype=jnp.int32)
    pool_rows = blocks // PB_DEV * POOL + slot_row.astype(jnp.int32)
    prefix = cache_pool[holder_row.astype(jnp.int32), pool_rows].reshape(PMAX, LAT).astype(jnp.float32)
    suffix = suffix_group.reshape(SUF, LAT).astype(jnp.float32)
    queries = query_group.reshape(SUF, HEADS, LAT).astype(jnp.float32)
    pre_scores = jnp.einsum('thc,kc->htk', queries, prefix) * score_scale
    suf_scores = jnp.einsum('thc,kc->htk', queries, suffix) * score_scale
    key_index = jnp.arange(PMAX, dtype=jnp.int32)
    pre_scores = jnp.where(key_index[None, None, :] < length, pre_scores, -1e+30)
    causal = jnp.arange(SUF)[None, :] <= jnp.arange(SUF)[:, None]
    suf_scores = jnp.where(causal[None, :, :], suf_scores, -1e+30)
    highest = jnp.maximum(lax.optimization_barrier(jnp.max(pre_scores, axis=2)), lax.optimization_barrier(jnp.max(suf_scores, axis=2)))
    pre_exps = jnp.exp(pre_scores - highest[:, :, None])
    suf_exps = jnp.exp(suf_scores - highest[:, :, None])
    denominator = lax.optimization_barrier(jnp.sum(pre_exps, axis=2)) + lax.optimization_barrier(jnp.sum(suf_exps, axis=2))
    latent = jnp.einsum('htk,kc->thc', rounded(pre_exps), prefix[:, :KVR])
    latent = latent + jnp.einsum('htk,kc->thc', rounded(suf_exps), suffix[:, :KVR])
    latent = rounded(latent / jnp.transpose(denominator)[:, :, None])
    head_values = jnp.einsum('thc,hcv->thv', latent, w_value.astype(jnp.float32)).astype(jnp.bfloat16)
    return jnp.dot(head_values.reshape(SUF, HEADS * VDIM), w_out, preferred_element_type=jnp.float32)

def reference(queries, suffix_latent, cache_pool, holders, block_slots, prefix_len, hidden, w_value, w_out, norm_gain, experts, gate_weights, w_gate, w_up, w_down):

    def one_group(group_items):
        query_group, suffix_group, holder_row, slot_row, length = group_items
        return group_attention(query_group, suffix_group, holder_row, slot_row, length, cache_pool, w_value, w_out)
    attention = lax.map(one_group, (queries, suffix_latent, holders, block_slots, prefix_len))
    residual = hidden.astype(jnp.float32) + attention
    scale_rows = lax.rsqrt(lax.optimization_barrier(jnp.mean(residual * residual, axis=2, keepdims=True)) + norm_eps)
    normed = (residual * scale_rows * norm_gain.astype(jnp.float32)).astype(jnp.bfloat16)
    flat_tokens = normed.reshape(GROUPS * SUF, D)
    flat_choice = experts.reshape(GROUPS * SUF, TOP)
    flat_gates = gate_weights.reshape(GROUPS * SUF, TOP).astype(jnp.float32)
    slot_limit = N_REP * N_EP * CAP

    def one_expert(mixture, expert):
        is_named = flat_choice == expert
        picked = jnp.any(is_named, axis=1)
        row_index = jnp.nonzero(picked, size=slot_limit, fill_value=0)[0].astype(jnp.int32)
        filled = jnp.arange(slot_limit, dtype=jnp.int32) < jnp.sum(picked.astype(jnp.int32))
        weight = lax.optimization_barrier(jnp.sum(jnp.where(is_named, flat_gates, jnp.zeros_like(flat_gates)), axis=1))[row_index]
        weight = jnp.where(filled, weight, jnp.zeros_like(weight))
        token_rows = flat_tokens[row_index]
        gate_part = jnp.dot(token_rows, w_gate[expert], preferred_element_type=jnp.float32)
        up_part = jnp.dot(token_rows, w_up[expert], preferred_element_type=jnp.float32)
        units = (jax.nn.silu(gate_part) * up_part).astype(jnp.bfloat16)
        down_rows = w_down[expert]

        def add_slice(slice_index, running):
            unit_piece = lax.dynamic_slice_in_dim(units, slice_index * FF_DEV, FF_DEV, 1)
            down_part = lax.dynamic_slice_in_dim(down_rows, slice_index * FF_DEV, FF_DEV, 0)
            return running + rounded(jnp.dot(unit_piece, down_part, preferred_element_type=jnp.float32))
        summed = lax.fori_loop(0, N_REP, add_slice, jnp.zeros((slot_limit, D), jnp.float32))
        return (mixture.at[row_index].add(weight[:, None] * summed), None)
    mixture, unused = lax.scan(one_expert, jnp.zeros((GROUPS * SUF, D), jnp.float32), jnp.arange(EXPERTS, dtype=jnp.int32))
    return residual + mixture.reshape(GROUPS, SUF, D)
```

```python
import jax
import jax.numpy as jnp
from jax import lax
from jax.sharding import PartitionSpec as P

KVR = 512
ROPE = 64
SUF = 128


score_scale = 0.07216878364870323
norm_eps = 1e-06


def expert_units(token_rows, gate_rows, up_rows):
    gate_part = jnp.dot(token_rows, gate_rows, preferred_element_type=jnp.float32)
    up_part = jnp.dot(token_rows, up_rows, preferred_element_type=jnp.float32)
    return (jax.nn.silu(gate_part) * up_part).astype(jnp.bfloat16)


def local(
    queries,
    suffix_latent,
    cache_pool,
    holders,
    block_slots,
    prefix_len,
    hidden,
    w_value,
    w_out,
    norm_gain,
    experts,
    gate_weights,
    w_gate,
    w_up,
    w_down,
):
    rep_count = lax.axis_size("rep")
    ep_count = lax.axis_size("ep")
    rep_index = lax.axis_index("rep")
    ep_index = lax.axis_index("ep")
    pool_count = cache_pool.shape[1]
    block_width = cache_pool.shape[2]
    per_device = holders.shape[1] // ep_count
    per_holder = (per_device + rep_count - 1) // rep_count
    latent_width = KVR + ROPE
    mine_holders = lax.dynamic_slice_in_dim(holders, ep_index * per_device, per_device, 1)
    mine_slots = lax.dynamic_slice_in_dim(block_slots, ep_index * per_device, per_device, 1)
    position = jnp.arange(per_device, dtype=jnp.int32)
    same_holder = mine_holders[:, :, None] == mine_holders[:, None, :]
    earlier = position[None, :] < position[:, None]
    occurrence = jnp.sum((same_holder & earlier[None, :, :]).astype(jnp.int32), axis=2)
    wanted = mine_holders == rep_index
    chosen_slot = occurrence[:, :, None] == jnp.arange(per_holder, dtype=jnp.int32)[None, None, :]
    chosen_row = mine_slots[:, :, None] == jnp.arange(pool_count, dtype=jnp.int32)[None, None, :]
    selector = jnp.einsum(
        "son,soh->snh",
        (wanted[:, :, None] & chosen_slot).astype(jnp.float32),
        chosen_row.astype(jnp.float32),
        precision=lax.Precision.HIGHEST,
    )
    outgoing = jnp.dot(
        selector.reshape(rep_count * per_holder, pool_count).astype(jnp.bfloat16),
        cache_pool[0],
        preferred_element_type=jnp.float32,
    )
    outgoing = outgoing.astype(jnp.bfloat16).reshape(rep_count, per_holder, block_width)
    incoming = lax.all_to_all(outgoing, "rep", split_axis=0, concat_axis=0, tiled=True)
    own_holders = lax.dynamic_index_in_dim(mine_holders, rep_index, 0, keepdims=False)
    own_order = lax.dynamic_index_in_dim(occurrence, rep_index, 0, keepdims=False)
    source = own_holders * per_holder + own_order
    picker = (
        source[:, None] == jnp.arange(rep_count * per_holder, dtype=jnp.int32)[None, :]
    ).astype(jnp.bfloat16)
    own_blocks = jnp.dot(
        picker,
        incoming.reshape(rep_count * per_holder, block_width),
        preferred_element_type=jnp.float32,
    ).astype(jnp.bfloat16)
    prefix_width = own_blocks.shape[0] * block_width
    packed = jnp.concatenate([own_blocks.reshape(1, prefix_width), suffix_latent], axis=1)
    gathered = lax.all_gather(packed, "ep", axis=0, tiled=True)
    prefix_all = gathered[:, :prefix_width]
    suffix_all = gathered[:, prefix_width:]
    prefix_keys = prefix_all.reshape(-1, latent_width)
    suffix_keys = suffix_all.reshape(-1, latent_width)
    query_rows = queries[0].reshape(SUF, -1, latent_width)
    pre_scores = (
        jnp.einsum("thc,kc->htk", query_rows, prefix_keys, preferred_element_type=jnp.float32)
        * score_scale
    )
    suf_scores = (
        jnp.einsum("thc,kc->htk", query_rows, suffix_keys, preferred_element_type=jnp.float32)
        * score_scale
    )
    key_index = jnp.arange(prefix_keys.shape[0], dtype=jnp.int32)
    pre_scores = jnp.where(key_index[None, None, :] < prefix_len[0], pre_scores, -1e30)
    causal = jnp.arange(SUF)[None, :] <= jnp.arange(SUF)[:, None]
    suf_scores = jnp.where(causal[None, :, :], suf_scores, -1e30)
    highest = jnp.maximum(jnp.max(pre_scores, axis=2), jnp.max(suf_scores, axis=2))
    pre_exps = jnp.exp(pre_scores - highest[:, :, None])
    suf_exps = jnp.exp(suf_scores - highest[:, :, None])
    denominator = jnp.sum(pre_exps, axis=2) + jnp.sum(suf_exps, axis=2)
    latent = jnp.einsum(
        "htk,kc->thc",
        pre_exps.astype(jnp.bfloat16),
        prefix_keys[:, :KVR],
        preferred_element_type=jnp.float32,
    )
    latent = latent + jnp.einsum(
        "htk,kc->thc",
        suf_exps.astype(jnp.bfloat16),
        suffix_keys[:, :KVR],
        preferred_element_type=jnp.float32,
    )
    latent = (latent / jnp.transpose(denominator)[:, :, None]).astype(jnp.bfloat16)
    head_values = jnp.einsum(
        "thc,hcv->thv", latent, w_value, preferred_element_type=jnp.float32
    ).astype(jnp.bfloat16)
    head_values = head_values.reshape(SUF, -1)
    partial = jnp.dot(head_values, w_out, preferred_element_type=jnp.float32)
    partial = partial.reshape(ep_count, SUF // ep_count, -1)
    attention = jnp.sum(lax.all_to_all(partial, "ep", 0, 0, tiled=True), axis=0)
    residual = hidden[0].astype(jnp.float32) + attention
    scale_rows = lax.rsqrt(jnp.mean(residual * residual, axis=1, keepdims=True) + norm_eps)
    normed = (residual * scale_rows * norm_gain.astype(jnp.float32)).astype(jnp.bfloat16)
    tok_count = hidden.shape[1]
    chosen = experts[0]
    top_count = chosen.shape[1]
    expert_count = ep_count * w_gate.shape[0]
    capacity = min(tok_count, 2 * max(1, tok_count * top_count // expert_count))
    slot_count = expert_count * capacity
    flat_choice = chosen.reshape(-1)
    hits = (flat_choice[:, None] == jnp.arange(expert_count, dtype=jnp.int32)[None, :]).astype(
        jnp.int32
    )
    rank = jnp.sum((jnp.cumsum(hits, axis=0) - hits) * hits, axis=1)
    slot_id = flat_choice * capacity + rank
    slot_hot = (slot_id[:, None] == jnp.arange(slot_count, dtype=jnp.int32)[None, :]).astype(
        jnp.float32
    )
    owner = jnp.arange(flat_choice.shape[0], dtype=jnp.int32) // top_count
    token_hot = (owner[:, None] == jnp.arange(tok_count, dtype=jnp.int32)[None, :]).astype(
        jnp.float32
    )
    placing = jnp.dot(jnp.transpose(slot_hot), token_hot, precision=lax.Precision.HIGHEST)
    weighted_hot = token_hot * gate_weights[0].astype(jnp.float32).reshape(-1)[:, None]
    combine = jnp.dot(jnp.transpose(weighted_hot), slot_hot, precision=lax.Precision.HIGHEST)
    grouped = jnp.dot(
        placing.astype(jnp.bfloat16), normed, preferred_element_type=jnp.float32
    ).astype(jnp.bfloat16)
    grouped = grouped.reshape(expert_count, capacity, -1)
    mine = lax.all_to_all(grouped, "ep", split_axis=0, concat_axis=0, tiled=True)
    copies = jnp.broadcast_to(mine[None], (rep_count,) + mine.shape)
    batch = lax.all_to_all(copies, "rep", split_axis=0, concat_axis=0, tiled=True)
    units = expert_units(batch.reshape(-1, batch.shape[-1]), w_gate[0], w_up[0])
    outputs = jnp.dot(units, w_down[0], preferred_element_type=jnp.float32).astype(jnp.bfloat16)
    back = lax.all_to_all(outputs.reshape(batch.shape), "rep", split_axis=0, concat_axis=0, tiled=True)
    slice_sum = jnp.sum(back.astype(jnp.float32), axis=0)
    served = lax.all_to_all(slice_sum, "ep", split_axis=0, concat_axis=0, tiled=True)
    mixture = jnp.dot(
        combine, served.reshape(slot_count, -1), precision=lax.Precision.HIGHEST
    )
    return (residual + mixture)[None]


def solution(mesh):
    return jax.shard_map(
        local,
        mesh=mesh,
        in_specs=(
            P("rep", None, "ep"),
            P("rep", "ep"),
            P("rep", "ep", None),
            P(),
            P(),
            P("rep"),
            P("rep", "ep", None),
            P("ep", None, None),
            P("ep", None),
            P(),
            P("rep", "ep", None),
            P("rep", "ep", None),
            P("ep", None, "rep"),
            P("ep", None, "rep"),
            P("ep", "rep", None),
        ),
        out_specs=P("rep", "ep", None),
        check_vma=False,
    )
```

```python
import jax
import jax.numpy as jnp
from jax import lax
from jax.sharding import Mesh, PartitionSpec as P

KVR = 512
ROPE = 64
SUF = 128
EP = ("epo", "core")


score_scale = 0.07216878364870323
norm_eps = 1e-06


def expert_units(token_rows, gate_rows, up_rows):
    gate_part = jnp.dot(token_rows, gate_rows, preferred_element_type=jnp.float32)
    up_part = jnp.dot(token_rows, up_rows, preferred_element_type=jnp.float32)
    return (jax.nn.silu(gate_part) * up_part).astype(jnp.bfloat16)


def local(
    queries,
    suffix_latent,
    cache_pool,
    holders,
    block_slots,
    prefix_len,
    hidden,
    w_value,
    w_out,
    norm_gain,
    experts,
    gate_weights,
    w_gate,
    w_up,
    w_down,
):
    rep_count = lax.axis_size("rep")
    ep_count = lax.axis_size(EP)
    rep_index = lax.axis_index("rep")
    ep_index = lax.axis_index("epo") * lax.axis_size("core") + lax.axis_index("core")
    pool_count = cache_pool.shape[1]
    block_width = cache_pool.shape[2]
    per_device = holders.shape[1] // ep_count
    per_holder = (per_device + rep_count - 1) // rep_count
    latent_width = KVR + ROPE
    mine_holders = lax.dynamic_slice_in_dim(holders, ep_index * per_device, per_device, 1)
    mine_slots = lax.dynamic_slice_in_dim(block_slots, ep_index * per_device, per_device, 1)
    position = jnp.arange(per_device, dtype=jnp.int32)
    same_holder = mine_holders[:, :, None] == mine_holders[:, None, :]
    earlier = position[None, :] < position[:, None]
    occurrence = jnp.sum((same_holder & earlier[None, :, :]).astype(jnp.int32), axis=2)
    wanted = mine_holders == rep_index
    chosen_slot = occurrence[:, :, None] == jnp.arange(per_holder, dtype=jnp.int32)[None, None, :]
    chosen_row = mine_slots[:, :, None] == jnp.arange(pool_count, dtype=jnp.int32)[None, None, :]
    selector = jnp.einsum(
        "son,soh->snh",
        (wanted[:, :, None] & chosen_slot).astype(jnp.float32),
        chosen_row.astype(jnp.float32),
        precision=lax.Precision.HIGHEST,
    )
    outgoing = jnp.dot(
        selector.reshape(rep_count * per_holder, pool_count).astype(jnp.bfloat16),
        cache_pool[0],
        preferred_element_type=jnp.float32,
    )
    outgoing = outgoing.astype(jnp.bfloat16).reshape(rep_count, per_holder, block_width)
    incoming = lax.all_to_all(outgoing, "rep", split_axis=0, concat_axis=0, tiled=True)
    own_holders = lax.dynamic_index_in_dim(mine_holders, rep_index, 0, keepdims=False)
    own_order = lax.dynamic_index_in_dim(occurrence, rep_index, 0, keepdims=False)
    source = own_holders * per_holder + own_order
    picker = (
        source[:, None] == jnp.arange(rep_count * per_holder, dtype=jnp.int32)[None, :]
    ).astype(jnp.bfloat16)
    own_blocks = jnp.dot(
        picker,
        incoming.reshape(rep_count * per_holder, block_width),
        preferred_element_type=jnp.float32,
    ).astype(jnp.bfloat16)
    prefix_width = own_blocks.shape[0] * block_width
    packed = jnp.concatenate([own_blocks.reshape(1, prefix_width), suffix_latent], axis=1)
    gathered = lax.all_gather(packed, EP, axis=0, tiled=True)
    prefix_all = gathered[:, :prefix_width]
    suffix_all = gathered[:, prefix_width:]
    prefix_keys = prefix_all.reshape(-1, latent_width)
    suffix_keys = suffix_all.reshape(-1, latent_width)
    query_rows = queries[0].reshape(SUF, -1, latent_width)
    pre_scores = (
        jnp.einsum("thc,kc->htk", query_rows, prefix_keys, preferred_element_type=jnp.float32)
        * score_scale
    )
    suf_scores = (
        jnp.einsum("thc,kc->htk", query_rows, suffix_keys, preferred_element_type=jnp.float32)
        * score_scale
    )
    key_index = jnp.arange(prefix_keys.shape[0], dtype=jnp.int32)
    pre_scores = jnp.where(key_index[None, None, :] < prefix_len[0], pre_scores, -1e30)
    causal = jnp.arange(SUF)[None, :] <= jnp.arange(SUF)[:, None]
    suf_scores = jnp.where(causal[None, :, :], suf_scores, -1e30)
    highest = jnp.maximum(jnp.max(pre_scores, axis=2), jnp.max(suf_scores, axis=2))
    pre_exps = jnp.exp(pre_scores - highest[:, :, None])
    suf_exps = jnp.exp(suf_scores - highest[:, :, None])
    denominator = jnp.sum(pre_exps, axis=2) + jnp.sum(suf_exps, axis=2)
    latent = jnp.einsum(
        "htk,kc->thc",
        pre_exps.astype(jnp.bfloat16),
        prefix_keys[:, :KVR],
        preferred_element_type=jnp.float32,
    )
    latent = latent + jnp.einsum(
        "htk,kc->thc",
        suf_exps.astype(jnp.bfloat16),
        suffix_keys[:, :KVR],
        preferred_element_type=jnp.float32,
    )
    latent = (latent / jnp.transpose(denominator)[:, :, None]).astype(jnp.bfloat16)
    head_values = jnp.einsum(
        "thc,hcv->thv", latent, w_value, preferred_element_type=jnp.float32
    ).astype(jnp.bfloat16)
    head_values = head_values.reshape(SUF, -1)
    partial = jnp.dot(head_values, w_out, preferred_element_type=jnp.float32)
    core_count = lax.axis_size("core")
    partial = partial.reshape(ep_count // core_count, core_count, -1)
    partial = jnp.sum(lax.all_to_all(partial, "core", 1, 1, tiled=True), axis=1)
    attention = jnp.sum(lax.all_to_all(partial, "epo", 0, 0, tiled=True), axis=0)
    attention = attention.reshape(SUF // ep_count, -1)
    residual = hidden[0].astype(jnp.float32) + attention
    scale_rows = lax.rsqrt(jnp.mean(residual * residual, axis=1, keepdims=True) + norm_eps)
    normed = (residual * scale_rows * norm_gain.astype(jnp.float32)).astype(jnp.bfloat16)
    tok_count = hidden.shape[1]
    chosen = experts[0]
    top_count = chosen.shape[1]
    expert_count = ep_count * w_gate.shape[0]
    capacity = min(tok_count, 2 * max(1, tok_count * top_count // expert_count))
    slot_count = expert_count * capacity
    flat_choice = chosen.reshape(-1)
    hits = (flat_choice[:, None] == jnp.arange(expert_count, dtype=jnp.int32)[None, :]).astype(
        jnp.int32
    )
    rank = jnp.sum((jnp.cumsum(hits, axis=0) - hits) * hits, axis=1)
    slot_id = flat_choice * capacity + rank
    slot_hot = (slot_id[:, None] == jnp.arange(slot_count, dtype=jnp.int32)[None, :]).astype(
        jnp.float32
    )
    owner = jnp.arange(flat_choice.shape[0], dtype=jnp.int32) // top_count
    token_hot = (owner[:, None] == jnp.arange(tok_count, dtype=jnp.int32)[None, :]).astype(
        jnp.float32
    )
    placing = jnp.dot(jnp.transpose(slot_hot), token_hot, precision=lax.Precision.HIGHEST)
    weighted_hot = token_hot * gate_weights[0].astype(jnp.float32).reshape(-1)[:, None]
    combine = jnp.dot(jnp.transpose(weighted_hot), slot_hot, precision=lax.Precision.HIGHEST)
    grouped = jnp.dot(
        placing.astype(jnp.bfloat16), normed, preferred_element_type=jnp.float32
    ).astype(jnp.bfloat16)
    width = grouped.shape[1]
    grouped = grouped.reshape(expert_count, capacity * width)
    mine = lax.all_to_all(grouped, EP, split_axis=0, concat_axis=0, tiled=True)
    mine = mine.reshape(slot_count, width)
    copies = jnp.broadcast_to(mine[None], (rep_count,) + mine.shape)
    batch = lax.all_to_all(copies, "rep", split_axis=0, concat_axis=0, tiled=True)
    units = expert_units(batch.reshape(-1, width), w_gate[0], w_up[0])
    outputs = jnp.dot(units, w_down[0], preferred_element_type=jnp.float32).astype(jnp.bfloat16)
    back = lax.all_to_all(outputs.reshape(batch.shape), "rep", split_axis=0, concat_axis=0, tiled=True)
    slice_sum = jnp.sum(back.astype(jnp.float32), axis=0).reshape(expert_count, capacity * width)
    served = lax.all_to_all(slice_sum, EP, split_axis=0, concat_axis=0, tiled=True)
    mixture = jnp.dot(
        combine, served.reshape(slot_count, width), precision=lax.Precision.HIGHEST
    )
    return (residual + mixture)[None]


def solution(mesh):
    rep_n, ep_n = mesh.devices.shape
    fine = Mesh(mesh.devices.reshape(rep_n, ep_n // 2, 2), ("rep", "epo", "core"))
    return jax.shard_map(
        local,
        mesh=fine,
        in_specs=(
            P("rep", None, EP),
            P("rep", EP),
            P("rep", EP, None),
            P(),
            P(),
            P("rep"),
            P("rep", EP, None),
            P(EP, None, None),
            P(EP, None),
            P(),
            P("rep", EP, None),
            P("rep", EP, None),
            P(EP, None, "rep"),
            P(EP, None, "rep"),
            P(EP, "rep", None),
        ),
        out_specs=P("rep", EP, None),
        check_vma=False,
    )
```

```python
import jax
import jax.numpy as jnp
from jax import lax
from jax.sharding import Mesh, PartitionSpec as P

KVR = 512
ROPE = 64
SUF = 128
EP = ("epo", "core")


score_scale = 0.07216878364870323
norm_eps = 1e-06


def expert_units(token_rows, gate_rows, up_rows):
    gate_part = jnp.dot(token_rows, gate_rows, preferred_element_type=jnp.float32)
    up_part = jnp.dot(token_rows, up_rows, preferred_element_type=jnp.float32)
    return (jax.nn.silu(gate_part) * up_part).astype(jnp.bfloat16)


def local(
    queries,
    suffix_latent,
    cache_pool,
    holders,
    block_slots,
    prefix_len,
    hidden,
    w_value,
    w_out,
    norm_gain,
    experts,
    gate_weights,
    w_gate,
    w_up,
    w_down,
):
    rep_count = lax.axis_size("rep")
    ep_count = lax.axis_size(EP)
    rep_index = lax.axis_index("rep")
    ep_index = lax.axis_index("epo") * lax.axis_size("core") + lax.axis_index("core")
    pool_count = cache_pool.shape[1]
    block_width = cache_pool.shape[2]
    per_device = holders.shape[1] // ep_count
    per_holder = (per_device + rep_count - 1) // rep_count
    latent_width = KVR + ROPE
    mine_holders = lax.dynamic_slice_in_dim(holders, ep_index * per_device, per_device, 1)
    mine_slots = lax.dynamic_slice_in_dim(block_slots, ep_index * per_device, per_device, 1)
    position = jnp.arange(per_device, dtype=jnp.int32)
    same_holder = mine_holders[:, :, None] == mine_holders[:, None, :]
    earlier = position[None, :] < position[:, None]
    occurrence = jnp.sum((same_holder & earlier[None, :, :]).astype(jnp.int32), axis=2)
    wanted = mine_holders == rep_index
    chosen_slot = occurrence[:, :, None] == jnp.arange(per_holder, dtype=jnp.int32)[None, None, :]
    chosen_row = mine_slots[:, :, None] == jnp.arange(pool_count, dtype=jnp.int32)[None, None, :]
    selector = jnp.einsum(
        "son,soh->snh",
        (wanted[:, :, None] & chosen_slot).astype(jnp.float32),
        chosen_row.astype(jnp.float32),
        precision=lax.Precision.HIGHEST,
    )
    outgoing = jnp.dot(
        selector.reshape(rep_count * per_holder, pool_count).astype(jnp.bfloat16),
        cache_pool[0],
        preferred_element_type=jnp.float32,
    )
    outgoing = outgoing.astype(jnp.bfloat16).reshape(rep_count, per_holder, block_width)
    incoming = lax.all_to_all(outgoing, "rep", split_axis=0, concat_axis=0, tiled=True)
    own_holders = lax.dynamic_index_in_dim(mine_holders, rep_index, 0, keepdims=False)
    own_order = lax.dynamic_index_in_dim(occurrence, rep_index, 0, keepdims=False)
    source = own_holders * per_holder + own_order
    picker = (
        source[:, None] == jnp.arange(rep_count * per_holder, dtype=jnp.int32)[None, :]
    ).astype(jnp.bfloat16)
    own_blocks = jnp.dot(
        picker,
        incoming.reshape(rep_count * per_holder, block_width),
        preferred_element_type=jnp.float32,
    ).astype(jnp.bfloat16)
    core_count = lax.axis_size("core")
    outer_count = ep_count // core_count
    pre_rows = per_device * (block_width // latent_width)
    suf_rows = SUF // ep_count
    pad_rows = -(pre_rows + suf_rows) % 16
    packed = jnp.concatenate(
        [
            own_blocks.reshape(pre_rows, latent_width),
            suffix_latent.reshape(suf_rows, latent_width),
            jnp.zeros((pad_rows, latent_width), own_blocks.dtype),
        ],
        axis=0,
    )
    row_count = packed.shape[0]
    chip_keys = lax.all_gather(packed[None], "epo", axis=0, tiled=True)
    chip_keys = jnp.broadcast_to(chip_keys[None], (core_count,) + chip_keys.shape)
    all_keys = lax.all_to_all(chip_keys, "core", 0, 0, tiled=True)
    keys = all_keys.reshape(-1, latent_width)
    core_of = lax.broadcasted_iota(jnp.int32, all_keys.shape[:3], 0)
    outer_of = lax.broadcasted_iota(jnp.int32, all_keys.shape[:3], 1)
    row_of = lax.broadcasted_iota(jnp.int32, all_keys.shape[:3], 2)
    device_of = (outer_of * core_count + core_of).reshape(-1)
    row_of = row_of.reshape(-1)
    is_prefix = (row_of < pre_rows) & (device_of * pre_rows + row_of < prefix_len[0])
    suffix_pos = device_of * suf_rows + row_of - pre_rows
    is_suffix = (row_of >= pre_rows) & (row_of < pre_rows + suf_rows)
    token_pos = jnp.arange(SUF, dtype=jnp.int32)
    visible = is_prefix[None, :] | (is_suffix[None, :] & (suffix_pos[None, :] <= token_pos[:, None]))
    query_rows = queries[0].reshape(SUF, -1, latent_width)
    scores = (
        jnp.einsum("thc,kc->htk", query_rows, keys, preferred_element_type=jnp.float32)
        * score_scale
    )
    scores = jnp.where(visible[None, :, :], scores, -1e30)
    highest = jnp.max(scores, axis=2)
    exps = jnp.exp(scores - highest[:, :, None])
    denominator = jnp.sum(exps, axis=2)
    latent = jnp.einsum(
        "htk,kc->thc",
        exps.astype(jnp.bfloat16),
        keys[:, :KVR],
        preferred_element_type=jnp.float32,
    )
    latent = (latent / jnp.transpose(denominator)[:, :, None]).astype(jnp.bfloat16)
    head_values = jnp.einsum(
        "thc,hcv->thv", latent, w_value, preferred_element_type=jnp.float32
    ).astype(jnp.bfloat16)
    head_values = head_values.reshape(outer_count, core_count, suf_rows, -1)
    head_values = jnp.transpose(head_values, (1, 0, 2, 3)).reshape(SUF, -1)
    partial = jnp.dot(head_values, w_out, preferred_element_type=jnp.float32)
    partial = partial.reshape(core_count, SUF // core_count, -1)
    partial = jnp.sum(lax.all_to_all(partial, "core", 0, 0, tiled=True), axis=0)
    partial = partial.reshape(outer_count, 8, -1)
    attention = jnp.sum(lax.all_to_all(partial, "epo", 0, 0, tiled=True), axis=0)
    attention = attention.reshape(suf_rows, -1)
    residual = hidden[0].astype(jnp.float32) + attention
    scale_rows = lax.rsqrt(jnp.mean(residual * residual, axis=1, keepdims=True) + norm_eps)
    normed = (residual * scale_rows * norm_gain.astype(jnp.float32)).astype(jnp.bfloat16)
    tok_count = hidden.shape[1]
    chosen = experts[0]
    top_count = chosen.shape[1]
    expert_count = ep_count * w_gate.shape[0]
    capacity = min(tok_count, 2 * max(1, tok_count * top_count // expert_count))
    slot_count = expert_count * capacity
    flat_choice = chosen.reshape(-1)
    hits = (flat_choice[:, None] == jnp.arange(expert_count, dtype=jnp.int32)[None, :]).astype(
        jnp.int32
    )
    rank = jnp.sum((jnp.cumsum(hits, axis=0) - hits) * hits, axis=1)
    slot_id = flat_choice * capacity + rank
    slot_hot = (slot_id[:, None] == jnp.arange(slot_count, dtype=jnp.int32)[None, :]).astype(
        jnp.float32
    )
    owner = jnp.arange(flat_choice.shape[0], dtype=jnp.int32) // top_count
    token_hot = (owner[:, None] == jnp.arange(tok_count, dtype=jnp.int32)[None, :]).astype(
        jnp.float32
    )
    placing = jnp.dot(jnp.transpose(slot_hot), token_hot, precision=lax.Precision.HIGHEST)
    weighted_hot = token_hot * gate_weights[0].astype(jnp.float32).reshape(-1)[:, None]
    combine = jnp.dot(jnp.transpose(weighted_hot), slot_hot, precision=lax.Precision.HIGHEST)
    grouped = jnp.dot(
        placing.astype(jnp.bfloat16), normed, preferred_element_type=jnp.float32
    ).astype(jnp.bfloat16)
    width = grouped.shape[1]
    grouped = grouped.reshape(expert_count, 16, -1)
    mine = lax.all_to_all(grouped, EP, split_axis=0, concat_axis=0, tiled=True)
    mine = mine.reshape(slot_count, width)
    copies = jnp.broadcast_to(mine[None], (rep_count,) + mine.shape)
    batch = lax.all_to_all(copies, "rep", split_axis=0, concat_axis=0, tiled=True)
    units = expert_units(batch.reshape(-1, width), w_gate[0], w_up[0])
    outputs = jnp.dot(units, w_down[0], preferred_element_type=jnp.float32).astype(jnp.bfloat16)
    back = lax.all_to_all(outputs.reshape(batch.shape), "rep", split_axis=0, concat_axis=0, tiled=True)
    slice_sum = jnp.sum(back.astype(jnp.float32), axis=0).reshape(expert_count, 8, -1)
    served = lax.all_to_all(slice_sum, EP, split_axis=0, concat_axis=0, tiled=True)
    mixture = jnp.dot(
        combine, served.reshape(slot_count, width), precision=lax.Precision.HIGHEST
    )
    return (residual + mixture)[None]


def solution(mesh):
    rep_n, ep_n = mesh.devices.shape
    fine = Mesh(mesh.devices.reshape(rep_n, ep_n // 2, 2), ("rep", "epo", "core"))
    return jax.shard_map(
        local,
        mesh=fine,
        in_specs=(
            P("rep", None, EP),
            P("rep", EP),
            P("rep", EP, None),
            P(),
            P(),
            P("rep"),
            P("rep", EP, None),
            P(EP, None, None),
            P(EP, None),
            P(),
            P("rep", EP, None),
            P("rep", EP, None),
            P(EP, None, "rep"),
            P(EP, None, "rep"),
            P(EP, "rep", None),
        ),
        out_specs=P("rep", EP, None),
        check_vma=False,
    )
```

```python
import jax
import jax.numpy as jnp
from jax import lax
from jax.sharding import Mesh, PartitionSpec as P

KVR = 512
ROPE = 64
SUF = 128
EP = ("epo", "core")


score_scale = 0.07216878364870323
norm_eps = 1e-06


def expert_units(token_rows, gate_rows, up_rows):
    gate_part = jnp.dot(token_rows, gate_rows, preferred_element_type=jnp.float32)
    up_part = jnp.dot(token_rows, up_rows, preferred_element_type=jnp.float32)
    return (jax.nn.silu(gate_part) * up_part).astype(jnp.bfloat16)


def local(
    queries,
    suffix_latent,
    cache_pool,
    holders,
    block_slots,
    prefix_len,
    hidden,
    w_value,
    w_out,
    norm_gain,
    experts,
    gate_weights,
    w_gate,
    w_up,
    w_down,
):
    rep_count = lax.axis_size("rep")
    ep_count = lax.axis_size(EP)
    rep_index = lax.axis_index("rep")
    ep_index = lax.axis_index("epo") * lax.axis_size("core") + lax.axis_index("core")
    pool_count = cache_pool.shape[1]
    block_width = cache_pool.shape[2]
    per_device = holders.shape[1] // ep_count
    per_holder = (per_device + rep_count - 1) // rep_count
    latent_width = KVR + ROPE
    mine_holders = lax.dynamic_slice_in_dim(holders, ep_index * per_device, per_device, 1)
    mine_slots = lax.dynamic_slice_in_dim(block_slots, ep_index * per_device, per_device, 1)
    position = jnp.arange(per_device, dtype=jnp.int32)
    same_holder = mine_holders[:, :, None] == mine_holders[:, None, :]
    earlier = position[None, :] < position[:, None]
    occurrence = jnp.sum((same_holder & earlier[None, :, :]).astype(jnp.int32), axis=2)
    wanted = mine_holders == rep_index
    chosen_slot = occurrence[:, :, None] == jnp.arange(per_holder, dtype=jnp.int32)[None, None, :]
    chosen_row = mine_slots[:, :, None] == jnp.arange(pool_count, dtype=jnp.int32)[None, None, :]
    selector = jnp.einsum(
        "son,soh->snh",
        (wanted[:, :, None] & chosen_slot).astype(jnp.float32),
        chosen_row.astype(jnp.float32),
        precision=lax.Precision.HIGHEST,
    )
    outgoing = jnp.dot(
        selector.reshape(rep_count * per_holder, pool_count).astype(jnp.bfloat16),
        cache_pool[0],
        preferred_element_type=jnp.float32,
    )
    outgoing = outgoing.astype(jnp.bfloat16).reshape(rep_count, per_holder, block_width)
    incoming = lax.all_to_all(outgoing, "rep", split_axis=0, concat_axis=0, tiled=True)
    own_holders = lax.dynamic_index_in_dim(mine_holders, rep_index, 0, keepdims=False)
    own_order = lax.dynamic_index_in_dim(occurrence, rep_index, 0, keepdims=False)
    source = own_holders * per_holder + own_order
    picker = (
        source[:, None] == jnp.arange(rep_count * per_holder, dtype=jnp.int32)[None, :]
    ).astype(jnp.bfloat16)
    own_blocks = jnp.dot(
        picker,
        incoming.reshape(rep_count * per_holder, block_width),
        preferred_element_type=jnp.float32,
    ).astype(jnp.bfloat16)
    core_count = lax.axis_size("core")
    outer_count = ep_count // core_count
    pre_rows = per_device * (block_width // latent_width)
    suf_rows = SUF // ep_count
    pad_rows = -(pre_rows + suf_rows) % 16
    packed = jnp.concatenate(
        [
            own_blocks.reshape(pre_rows, latent_width),
            suffix_latent.reshape(suf_rows, latent_width),
            jnp.zeros((pad_rows, latent_width), own_blocks.dtype),
        ],
        axis=0,
    )
    row_count = packed.shape[0]
    chip_keys = lax.all_gather(packed[None], "epo", axis=0, tiled=True)
    hidden_width, width = w_down.shape[1], w_down.shape[2]
    chunk = width // rep_count
    down_cols = w_down[0].reshape(hidden_width, rep_count, chunk)
    down_cols = jnp.transpose(down_cols, (1, 0, 2))
    down_cols = lax.all_to_all(down_cols, "rep", 0, 0, tiled=True)
    chip_keys, down_cols = lax.optimization_barrier((chip_keys, down_cols))
    chip_keys = jnp.broadcast_to(chip_keys[None], (core_count,) + chip_keys.shape)
    all_keys = lax.all_to_all(chip_keys, "core", 0, 0, tiled=True)
    keys = all_keys.reshape(-1, latent_width)
    core_of = lax.broadcasted_iota(jnp.int32, all_keys.shape[:3], 0)
    outer_of = lax.broadcasted_iota(jnp.int32, all_keys.shape[:3], 1)
    row_of = lax.broadcasted_iota(jnp.int32, all_keys.shape[:3], 2)
    device_of = (outer_of * core_count + core_of).reshape(-1)
    row_of = row_of.reshape(-1)
    is_prefix = (row_of < pre_rows) & (device_of * pre_rows + row_of < prefix_len[0])
    suffix_pos = device_of * suf_rows + row_of - pre_rows
    is_suffix = (row_of >= pre_rows) & (row_of < pre_rows + suf_rows)
    token_pos = jnp.arange(SUF, dtype=jnp.int32)
    visible = is_prefix[None, :] | (is_suffix[None, :] & (suffix_pos[None, :] <= token_pos[:, None]))
    query_rows = queries[0].reshape(SUF, -1, latent_width)
    scores = (
        jnp.einsum("thc,kc->htk", query_rows, keys, preferred_element_type=jnp.float32)
        * score_scale
    )
    scores = jnp.where(visible[None, :, :], scores, -1e30)
    highest = jnp.max(scores, axis=2)
    exps = jnp.exp(scores - highest[:, :, None])
    denominator = jnp.sum(exps, axis=2)
    latent = jnp.einsum(
        "htk,kc->thc",
        exps.astype(jnp.bfloat16),
        keys[:, :KVR],
        preferred_element_type=jnp.float32,
    )
    latent = (latent / jnp.transpose(denominator)[:, :, None]).astype(jnp.bfloat16)
    head_values = jnp.einsum(
        "thc,hcv->thv", latent, w_value, preferred_element_type=jnp.float32
    ).astype(jnp.bfloat16)
    head_values = head_values.reshape(outer_count, core_count, suf_rows, -1)
    head_values = jnp.transpose(head_values, (1, 0, 2, 3)).reshape(SUF, -1)
    partial = jnp.dot(head_values, w_out, preferred_element_type=jnp.float32)
    partial = partial.reshape(core_count, SUF // core_count, -1)
    partial = jnp.sum(lax.all_to_all(partial, "core", 0, 0, tiled=True), axis=0)
    partial = partial.reshape(outer_count, 8, -1)
    attention = jnp.sum(lax.all_to_all(partial, "epo", 0, 0, tiled=True), axis=0)
    attention = attention.reshape(suf_rows, -1)
    residual = hidden[0].astype(jnp.float32) + attention
    scale_rows = lax.rsqrt(jnp.mean(residual * residual, axis=1, keepdims=True) + norm_eps)
    normed = (residual * scale_rows * norm_gain.astype(jnp.float32)).astype(jnp.bfloat16)
    tok_count = hidden.shape[1]
    chosen = experts[0]
    top_count = chosen.shape[1]
    expert_count = ep_count * w_gate.shape[0]
    capacity = min(tok_count, 2 * max(1, tok_count * top_count // expert_count))
    slot_count = expert_count * capacity
    flat_choice = chosen.reshape(-1)
    hits = (flat_choice[:, None] == jnp.arange(expert_count, dtype=jnp.int32)[None, :]).astype(
        jnp.int32
    )
    rank = jnp.sum((jnp.cumsum(hits, axis=0) - hits) * hits, axis=1)
    slot_id = flat_choice * capacity + rank
    slot_hot = (slot_id[:, None] == jnp.arange(slot_count, dtype=jnp.int32)[None, :]).astype(
        jnp.float32
    )
    owner = jnp.arange(flat_choice.shape[0], dtype=jnp.int32) // top_count
    token_hot = (owner[:, None] == jnp.arange(tok_count, dtype=jnp.int32)[None, :]).astype(
        jnp.float32
    )
    placing = jnp.dot(jnp.transpose(slot_hot), token_hot, precision=lax.Precision.HIGHEST)
    weighted_hot = token_hot * gate_weights[0].astype(jnp.float32).reshape(-1)[:, None]
    combine = jnp.dot(jnp.transpose(weighted_hot), slot_hot, precision=lax.Precision.HIGHEST)
    grouped = jnp.dot(
        placing.astype(jnp.bfloat16), normed, preferred_element_type=jnp.float32
    ).astype(jnp.bfloat16)
    width = grouped.shape[1]
    grouped = grouped.reshape(expert_count, 16, -1)
    mine = lax.all_to_all(grouped, EP, split_axis=0, concat_axis=0, tiled=True)
    mine = mine.reshape(slot_count, width)
    copies = jnp.broadcast_to(mine[None], (rep_count,) + mine.shape)
    batch = lax.all_to_all(copies, "rep", split_axis=0, concat_axis=0, tiled=True)
    units = expert_units(batch.reshape(-1, width), w_gate[0], w_up[0])
    hidden_width = units.shape[1]
    unit_copies = jnp.broadcast_to(units[None], (rep_count,) + units.shape)
    units_all = lax.all_to_all(unit_copies, "rep", 0, 0, tiled=True)
    pieces = jnp.einsum("rnk,rkc->rnc", units_all, down_cols, preferred_element_type=jnp.float32)
    out_cols = jnp.sum(pieces.astype(jnp.bfloat16).astype(jnp.float32), axis=0)
    out_cols = out_cols.reshape(rep_count, slot_count, chunk)
    back = lax.all_to_all(out_cols, "rep", 0, 0, tiled=True)
    back = jnp.transpose(back, (1, 0, 2)).reshape(expert_count, capacity * rep_count, chunk)
    served = lax.all_to_all(back, EP, split_axis=0, concat_axis=0, tiled=True)
    mixture = jnp.dot(
        combine, served.reshape(slot_count, width), precision=lax.Precision.HIGHEST
    )
    return (residual + mixture)[None]


def solution(mesh):
    rep_n, ep_n = mesh.devices.shape
    fine = Mesh(mesh.devices.reshape(rep_n, ep_n // 2, 2), ("rep", "epo", "core"))
    return jax.shard_map(
        local,
        mesh=fine,
        in_specs=(
            P("rep", None, EP),
            P("rep", EP),
            P("rep", EP, None),
            P(),
            P(),
            P("rep"),
            P("rep", EP, None),
            P(EP, None, None),
            P(EP, None),
            P(),
            P("rep", EP, None),
            P("rep", EP, None),
            P(EP, None, "rep"),
            P(EP, None, "rep"),
            P(EP, "rep", None),
        ),
        out_specs=P("rep", EP, None),
        check_vma=False,
    )
```

```python
import jax
import jax.numpy as jnp
from jax import lax
from jax.sharding import Mesh, PartitionSpec as P

KVR = 512
ROPE = 64
SUF = 128
EP = ("z", "ylo", "core")


score_scale = 0.07216878364870323
norm_eps = 1e-06


def expert_units(token_rows, gate_rows, up_rows):
    gate_part = jnp.dot(token_rows, gate_rows, preferred_element_type=jnp.float32)
    up_part = jnp.dot(token_rows, up_rows, preferred_element_type=jnp.float32)
    return (jax.nn.silu(gate_part) * up_part).astype(jnp.bfloat16)


def local(
    queries,
    suffix_latent,
    cache_pool,
    holders,
    block_slots,
    prefix_len,
    hidden,
    w_value,
    w_out,
    norm_gain,
    experts,
    gate_weights,
    w_gate,
    w_up,
    w_down,
):
    rep_count = lax.axis_size("rep")
    ep_count = lax.axis_size(EP)
    rep_index = lax.axis_index("rep")
    ep_index = (lax.axis_index("z") * lax.axis_size("ylo") + lax.axis_index("ylo")) * lax.axis_size(
        "core"
    ) + lax.axis_index("core")
    pool_count = cache_pool.shape[1]
    block_width = cache_pool.shape[2]
    per_device = holders.shape[1] // ep_count
    per_holder = (per_device + rep_count - 1) // rep_count
    latent_width = KVR + ROPE
    mine_holders = lax.dynamic_slice_in_dim(holders, ep_index * per_device, per_device, 1)
    mine_slots = lax.dynamic_slice_in_dim(block_slots, ep_index * per_device, per_device, 1)
    position = jnp.arange(per_device, dtype=jnp.int32)
    same_holder = mine_holders[:, :, None] == mine_holders[:, None, :]
    earlier = position[None, :] < position[:, None]
    occurrence = jnp.sum((same_holder & earlier[None, :, :]).astype(jnp.int32), axis=2)
    wanted = mine_holders == rep_index
    chosen_slot = occurrence[:, :, None] == jnp.arange(per_holder, dtype=jnp.int32)[None, None, :]
    chosen_row = mine_slots[:, :, None] == jnp.arange(pool_count, dtype=jnp.int32)[None, None, :]
    selector = jnp.einsum(
        "son,soh->snh",
        (wanted[:, :, None] & chosen_slot).astype(jnp.float32),
        chosen_row.astype(jnp.float32),
        precision=lax.Precision.HIGHEST,
    )
    outgoing = jnp.dot(
        selector.reshape(rep_count * per_holder, pool_count).astype(jnp.bfloat16),
        cache_pool[0],
        preferred_element_type=jnp.float32,
    )
    outgoing = outgoing.astype(jnp.bfloat16).reshape(rep_count, per_holder, block_width)
    incoming = lax.all_to_all(outgoing, "rep", split_axis=0, concat_axis=0, tiled=True)
    own_holders = lax.dynamic_index_in_dim(mine_holders, rep_index, 0, keepdims=False)
    own_order = lax.dynamic_index_in_dim(occurrence, rep_index, 0, keepdims=False)
    source = own_holders * per_holder + own_order
    picker = (
        source[:, None] == jnp.arange(rep_count * per_holder, dtype=jnp.int32)[None, :]
    ).astype(jnp.bfloat16)
    own_blocks = jnp.dot(
        picker,
        incoming.reshape(rep_count * per_holder, block_width),
        preferred_element_type=jnp.float32,
    ).astype(jnp.bfloat16)
    core_count = lax.axis_size("core")
    outer_count = ep_count // core_count
    pre_rows = per_device * (block_width // latent_width)
    suf_rows = SUF // ep_count
    pad_rows = -(pre_rows + suf_rows) % 16
    packed = jnp.concatenate(
        [
            own_blocks.reshape(pre_rows, latent_width),
            suffix_latent.reshape(suf_rows, latent_width),
            jnp.zeros((pad_rows, latent_width), own_blocks.dtype),
        ],
        axis=0,
    )
    row_count = packed.shape[0]
    chip_keys = lax.all_gather(packed[None], ("z", "ylo"), axis=0, tiled=True)
    hidden_width, width = w_down.shape[1], w_down.shape[2]
    chunk = width // rep_count
    down_cols = w_down[0].reshape(hidden_width, rep_count, chunk)
    down_cols = jnp.transpose(down_cols, (1, 0, 2))
    down_cols = lax.all_to_all(down_cols, "rep", 0, 0, tiled=True)
    chip_keys, down_cols = lax.optimization_barrier((chip_keys, down_cols))
    chip_keys = jnp.broadcast_to(chip_keys[None], (core_count,) + chip_keys.shape)
    all_keys = lax.all_to_all(chip_keys, "core", 0, 0, tiled=True)
    keys = all_keys.reshape(-1, latent_width)
    core_of = lax.broadcasted_iota(jnp.int32, all_keys.shape[:3], 0)
    outer_of = lax.broadcasted_iota(jnp.int32, all_keys.shape[:3], 1)
    row_of = lax.broadcasted_iota(jnp.int32, all_keys.shape[:3], 2)
    device_of = (outer_of * core_count + core_of).reshape(-1)
    row_of = row_of.reshape(-1)
    is_prefix = (row_of < pre_rows) & (device_of * pre_rows + row_of < prefix_len[0])
    suffix_pos = device_of * suf_rows + row_of - pre_rows
    is_suffix = (row_of >= pre_rows) & (row_of < pre_rows + suf_rows)
    token_pos = jnp.arange(SUF, dtype=jnp.int32)
    visible = is_prefix[None, :] | (is_suffix[None, :] & (suffix_pos[None, :] <= token_pos[:, None]))
    query_rows = queries[0].reshape(SUF, -1, latent_width)
    scores = (
        jnp.einsum("thc,kc->htk", query_rows, keys, preferred_element_type=jnp.float32)
        * score_scale
    )
    scores = jnp.where(visible[None, :, :], scores, -1e30)
    highest = jnp.max(scores, axis=2)
    exps = jnp.exp(scores - highest[:, :, None])
    denominator = jnp.sum(exps, axis=2)
    latent = jnp.einsum(
        "htk,kc->thc",
        exps.astype(jnp.bfloat16),
        keys[:, :KVR],
        preferred_element_type=jnp.float32,
    )
    latent = (latent / jnp.transpose(denominator)[:, :, None]).astype(jnp.bfloat16)
    head_values = jnp.einsum(
        "thc,hcv->thv", latent, w_value, preferred_element_type=jnp.float32
    ).astype(jnp.bfloat16)
    z_count, pair_count = lax.axis_size("z"), lax.axis_size("ylo")
    head_values = head_values.reshape(z_count, pair_count, core_count, suf_rows, -1)
    head_values = jnp.transpose(head_values, (2, 1, 0, 3, 4)).reshape(SUF, -1)
    partial = jnp.dot(head_values, w_out, preferred_element_type=jnp.float32)
    partial = partial.reshape(core_count, SUF // core_count, -1)
    partial = jnp.sum(lax.all_to_all(partial, "core", 0, 0, tiled=True), axis=0)
    partial = partial.reshape(pair_count, SUF // core_count // pair_count, -1)
    partial = jnp.sum(lax.all_to_all(partial, "ylo", 0, 0, tiled=True), axis=0)
    partial = partial.reshape(z_count, 8, -1)
    attention = jnp.sum(lax.all_to_all(partial, "z", 0, 0, tiled=True), axis=0)
    attention = attention.reshape(suf_rows, -1)
    residual = hidden[0].astype(jnp.float32) + attention
    scale_rows = lax.rsqrt(jnp.mean(residual * residual, axis=1, keepdims=True) + norm_eps)
    normed = (residual * scale_rows * norm_gain.astype(jnp.float32)).astype(jnp.bfloat16)
    tok_count = hidden.shape[1]
    chosen = experts[0]
    top_count = chosen.shape[1]
    expert_count = ep_count * w_gate.shape[0]
    capacity = min(tok_count, 2 * max(1, tok_count * top_count // expert_count))
    slot_count = expert_count * capacity
    flat_choice = chosen.reshape(-1)
    hits = (flat_choice[:, None] == jnp.arange(expert_count, dtype=jnp.int32)[None, :]).astype(
        jnp.int32
    )
    rank = jnp.sum((jnp.cumsum(hits, axis=0) - hits) * hits, axis=1)
    slot_id = flat_choice * capacity + rank
    slot_hot = (slot_id[:, None] == jnp.arange(slot_count, dtype=jnp.int32)[None, :]).astype(
        jnp.float32
    )
    owner = jnp.arange(flat_choice.shape[0], dtype=jnp.int32) // top_count
    token_hot = (owner[:, None] == jnp.arange(tok_count, dtype=jnp.int32)[None, :]).astype(
        jnp.float32
    )
    placing = jnp.dot(jnp.transpose(slot_hot), token_hot, precision=lax.Precision.HIGHEST)
    weighted_hot = token_hot * gate_weights[0].astype(jnp.float32).reshape(-1)[:, None]
    combine = jnp.dot(jnp.transpose(weighted_hot), slot_hot, precision=lax.Precision.HIGHEST)
    grouped = jnp.dot(
        placing.astype(jnp.bfloat16), normed, preferred_element_type=jnp.float32
    ).astype(jnp.bfloat16)
    width = grouped.shape[1]
    grouped = grouped.reshape(expert_count, 16, -1)
    mine = lax.all_to_all(grouped, EP, split_axis=0, concat_axis=0, tiled=True)
    mine = mine.reshape(slot_count, width)
    copies = jnp.broadcast_to(mine[None], (rep_count,) + mine.shape)
    batch = lax.all_to_all(copies, "rep", split_axis=0, concat_axis=0, tiled=True)
    units = expert_units(batch.reshape(-1, width), w_gate[0], w_up[0])
    hidden_width = units.shape[1]
    unit_copies = jnp.broadcast_to(units[None], (rep_count,) + units.shape)
    units_all = lax.all_to_all(unit_copies, "rep", 0, 0, tiled=True)
    pieces = jnp.einsum("rnk,rkc->rnc", units_all, down_cols, preferred_element_type=jnp.float32)
    out_cols = jnp.sum(pieces.astype(jnp.bfloat16).astype(jnp.float32), axis=0)
    out_cols = out_cols.reshape(rep_count, slot_count, chunk)
    back = lax.all_to_all(out_cols, "rep", 0, 0, tiled=True)
    back = jnp.transpose(back, (1, 0, 2)).reshape(expert_count, capacity * rep_count, chunk)
    served = lax.all_to_all(back, EP, split_axis=0, concat_axis=0, tiled=True)
    mixture = jnp.dot(
        combine, served.reshape(slot_count, width), precision=lax.Precision.HIGHEST
    )
    return (residual + mixture)[None]


def solution(mesh):
    rep_n, ep_n = mesh.devices.shape
    fine = Mesh(mesh.devices.reshape(rep_n, ep_n // 4, 2, 2), ("rep", "z", "ylo", "core"))
    return jax.shard_map(
        local,
        mesh=fine,
        in_specs=(
            P("rep", None, EP),
            P("rep", EP),
            P("rep", EP, None),
            P(),
            P(),
            P("rep"),
            P("rep", EP, None),
            P(EP, None, None),
            P(EP, None),
            P(),
            P("rep", EP, None),
            P("rep", EP, None),
            P(EP, None, "rep"),
            P(EP, None, "rep"),
            P(EP, "rep", None),
        ),
        out_specs=P("rep", EP, None),
        check_vma=False,
    )
```

```python
import jax
import jax.numpy as jnp
from jax import lax
from jax.sharding import Mesh, PartitionSpec as P

KVR = 512
ROPE = 64
SUF = 128
EP = ("epo", "core")


score_scale = 0.07216878364870323
norm_eps = 1e-06


def expert_units(token_rows, gate_rows, up_rows):
    gate_part = jnp.dot(token_rows, gate_rows, preferred_element_type=jnp.float32)
    up_part = jnp.dot(token_rows, up_rows, preferred_element_type=jnp.float32)
    return (jax.nn.silu(gate_part) * up_part).astype(jnp.bfloat16)


def local(
    queries,
    suffix_latent,
    cache_pool,
    holders,
    block_slots,
    prefix_len,
    hidden,
    w_value,
    w_out,
    norm_gain,
    experts,
    gate_weights,
    w_gate,
    w_up,
    w_down,
):
    rep_count = lax.axis_size("rep")
    ep_count = lax.axis_size(EP)
    rep_index = lax.axis_index("rep")
    ep_index = lax.axis_index("epo") * lax.axis_size("core") + lax.axis_index("core")
    pool_count = cache_pool.shape[1]
    block_width = cache_pool.shape[2]
    per_device = holders.shape[1] // ep_count
    per_holder = (per_device + rep_count - 1) // rep_count
    latent_width = KVR + ROPE
    mine_holders = lax.dynamic_slice_in_dim(holders, ep_index * per_device, per_device, 1)
    mine_slots = lax.dynamic_slice_in_dim(block_slots, ep_index * per_device, per_device, 1)
    position = jnp.arange(per_device, dtype=jnp.int32)
    same_holder = mine_holders[:, :, None] == mine_holders[:, None, :]
    earlier = position[None, :] < position[:, None]
    occurrence = jnp.sum((same_holder & earlier[None, :, :]).astype(jnp.int32), axis=2)
    wanted = mine_holders == rep_index
    chosen_slot = occurrence[:, :, None] == jnp.arange(per_holder, dtype=jnp.int32)[None, None, :]
    chosen_row = mine_slots[:, :, None] == jnp.arange(pool_count, dtype=jnp.int32)[None, None, :]
    selector = jnp.einsum(
        "son,soh->snh",
        (wanted[:, :, None] & chosen_slot).astype(jnp.float32),
        chosen_row.astype(jnp.float32),
        precision=lax.Precision.HIGHEST,
    )
    outgoing = jnp.dot(
        selector.reshape(rep_count * per_holder, pool_count).astype(jnp.bfloat16),
        cache_pool[0],
        preferred_element_type=jnp.float32,
    )
    outgoing = outgoing.astype(jnp.bfloat16).reshape(rep_count, per_holder, block_width)
    incoming = lax.all_to_all(outgoing, "rep", split_axis=0, concat_axis=0, tiled=True)
    own_holders = lax.dynamic_index_in_dim(mine_holders, rep_index, 0, keepdims=False)
    own_order = lax.dynamic_index_in_dim(occurrence, rep_index, 0, keepdims=False)
    source = own_holders * per_holder + own_order
    picker = (
        source[:, None] == jnp.arange(rep_count * per_holder, dtype=jnp.int32)[None, :]
    ).astype(jnp.bfloat16)
    own_blocks = jnp.dot(
        picker,
        incoming.reshape(rep_count * per_holder, block_width),
        preferred_element_type=jnp.float32,
    ).astype(jnp.bfloat16)
    core_count = lax.axis_size("core")
    outer_count = ep_count // core_count
    pre_rows = per_device * (block_width // latent_width)
    suf_rows = SUF // ep_count
    pad_rows = -(pre_rows + suf_rows) % 16
    packed = jnp.concatenate(
        [
            own_blocks.reshape(pre_rows, latent_width),
            suffix_latent.reshape(suf_rows, latent_width),
            jnp.zeros((pad_rows, latent_width), own_blocks.dtype),
        ],
        axis=0,
    )
    row_count = packed.shape[0]
    chip_keys = lax.all_gather(packed[None], "epo", axis=0, tiled=True)
    hidden_width, width = w_down.shape[1], w_down.shape[2]
    chunk = width // rep_count
    down_cols = w_down[0].reshape(hidden_width, rep_count, chunk)
    down_cols = jnp.transpose(down_cols, (1, 0, 2))
    down_cols = lax.all_to_all(down_cols, "rep", 0, 0, tiled=True)
    chip_keys, down_cols = lax.optimization_barrier((chip_keys, down_cols))
    chip_keys = jnp.broadcast_to(chip_keys[None], (core_count,) + chip_keys.shape)
    all_keys = lax.all_to_all(chip_keys, "core", 0, 0, tiled=True)
    keys = all_keys.reshape(-1, latent_width)
    core_of = lax.broadcasted_iota(jnp.int32, all_keys.shape[:3], 0)
    outer_of = lax.broadcasted_iota(jnp.int32, all_keys.shape[:3], 1)
    row_of = lax.broadcasted_iota(jnp.int32, all_keys.shape[:3], 2)
    device_of = (outer_of * core_count + core_of).reshape(-1)
    row_of = row_of.reshape(-1)
    is_prefix = (row_of < pre_rows) & (device_of * pre_rows + row_of < prefix_len[0])
    suffix_pos = device_of * suf_rows + row_of - pre_rows
    is_suffix = (row_of >= pre_rows) & (row_of < pre_rows + suf_rows)
    token_pos = jnp.arange(SUF, dtype=jnp.int32)
    visible = is_prefix[None, :] | (is_suffix[None, :] & (suffix_pos[None, :] <= token_pos[:, None]))
    query_rows = queries[0].reshape(SUF, -1, latent_width)
    scores = (
        jnp.einsum("thc,kc->htk", query_rows, keys, preferred_element_type=jnp.float32)
        * score_scale
    )
    scores = jnp.where(visible[None, :, :], scores, -1e30)
    highest = jnp.max(scores, axis=2)
    exps = jnp.exp(scores - highest[:, :, None])
    denominator = jnp.sum(exps, axis=2)
    latent = jnp.einsum(
        "htk,kc->thc",
        exps.astype(jnp.bfloat16),
        keys[:, :KVR],
        preferred_element_type=jnp.float32,
    )
    latent = (latent / jnp.transpose(denominator)[:, :, None]).astype(jnp.bfloat16)
    head_values = jnp.einsum(
        "thc,hcv->thv", latent, w_value, preferred_element_type=jnp.float32
    ).astype(jnp.bfloat16)
    head_values = head_values.reshape(outer_count, core_count, suf_rows, -1)
    head_values = jnp.transpose(head_values, (1, 0, 2, 3)).reshape(SUF, -1)
    partial = jnp.dot(head_values, w_out, preferred_element_type=jnp.float32)
    partial = partial.reshape(core_count, SUF // core_count, -1)
    partial = jnp.sum(lax.all_to_all(partial, "core", 0, 0, tiled=True), axis=0)
    partial = partial.reshape(outer_count, 16, -1).astype(jnp.bfloat16)
    attention = jnp.sum(
        lax.all_to_all(partial, "epo", 0, 0, tiled=True).astype(jnp.float32), axis=0
    )
    attention = attention.reshape(suf_rows, -1)
    residual = hidden[0].astype(jnp.float32) + attention
    scale_rows = lax.rsqrt(jnp.mean(residual * residual, axis=1, keepdims=True) + norm_eps)
    normed = (residual * scale_rows * norm_gain.astype(jnp.float32)).astype(jnp.bfloat16)
    tok_count = hidden.shape[1]
    chosen = experts[0]
    top_count = chosen.shape[1]
    expert_count = ep_count * w_gate.shape[0]
    capacity = min(tok_count, 2 * max(1, tok_count * top_count // expert_count))
    slot_count = expert_count * capacity
    flat_choice = chosen.reshape(-1)
    hits = (flat_choice[:, None] == jnp.arange(expert_count, dtype=jnp.int32)[None, :]).astype(
        jnp.int32
    )
    rank = jnp.sum((jnp.cumsum(hits, axis=0) - hits) * hits, axis=1)
    slot_id = flat_choice * capacity + rank
    slot_hot = (slot_id[:, None] == jnp.arange(slot_count, dtype=jnp.int32)[None, :]).astype(
        jnp.float32
    )
    owner = jnp.arange(flat_choice.shape[0], dtype=jnp.int32) // top_count
    token_hot = (owner[:, None] == jnp.arange(tok_count, dtype=jnp.int32)[None, :]).astype(
        jnp.float32
    )
    placing = jnp.dot(jnp.transpose(slot_hot), token_hot, precision=lax.Precision.HIGHEST)
    weighted_hot = token_hot * gate_weights[0].astype(jnp.float32).reshape(-1)[:, None]
    combine = jnp.dot(jnp.transpose(weighted_hot), slot_hot, precision=lax.Precision.HIGHEST)
    grouped = jnp.dot(
        placing.astype(jnp.bfloat16), normed, preferred_element_type=jnp.float32
    ).astype(jnp.bfloat16)
    width = grouped.shape[1]
    grouped = grouped.reshape(expert_count, 16, -1)
    mine = lax.all_to_all(grouped, EP, split_axis=0, concat_axis=0, tiled=True)
    mine = mine.reshape(slot_count, width)
    copies = jnp.broadcast_to(mine[None], (rep_count,) + mine.shape)
    batch = lax.all_to_all(copies, "rep", split_axis=0, concat_axis=0, tiled=True)
    units = expert_units(batch.reshape(-1, width), w_gate[0], w_up[0])
    hidden_width = units.shape[1]
    unit_copies = jnp.broadcast_to(units[None], (rep_count,) + units.shape)
    units_all = lax.all_to_all(unit_copies, "rep", 0, 0, tiled=True)
    pieces = jnp.einsum("rnk,rkc->rnc", units_all, down_cols, preferred_element_type=jnp.float32)
    out_cols = jnp.sum(pieces.astype(jnp.bfloat16).astype(jnp.float32), axis=0)
    out_cols = out_cols.astype(jnp.bfloat16)
    out_cols = out_cols.reshape(rep_count, slot_count, chunk)
    back = lax.all_to_all(out_cols, "rep", 0, 0, tiled=True)
    back = jnp.transpose(back, (1, 0, 2)).reshape(expert_count, capacity * rep_count, chunk)
    served = lax.all_to_all(back, EP, split_axis=0, concat_axis=0, tiled=True)
    mixture = jnp.dot(
        combine, served.reshape(slot_count, width).astype(jnp.float32), precision=lax.Precision.HIGHEST
    )
    return (residual + mixture)[None]


def solution(mesh):
    rep_n, ep_n = mesh.devices.shape
    fine = Mesh(mesh.devices.reshape(rep_n, ep_n // 2, 2), ("rep", "epo", "core"))
    return jax.shard_map(
        local,
        mesh=fine,
        in_specs=(
            P("rep", None, EP),
            P("rep", EP),
            P("rep", EP, None),
            P(),
            P(),
            P("rep"),
            P("rep", EP, None),
            P(EP, None, None),
            P(EP, None),
            P(),
            P("rep", EP, None),
            P("rep", EP, None),
            P(EP, None, "rep"),
            P(EP, None, "rep"),
            P(EP, "rep", None),
        ),
        out_specs=P("rep", EP, None),
        check_vma=False,
    )
```

```python
import jax
import jax.numpy as jnp
from jax import lax
from jax.sharding import Mesh, PartitionSpec as P

KVR = 512
ROPE = 64
SUF = 128
EP = ("epo", "core")


score_scale = 0.07216878364870323
norm_eps = 1e-06


def expert_units(token_rows, gate_rows, up_rows):
    gate_part = jnp.dot(token_rows, gate_rows, preferred_element_type=jnp.float32)
    up_part = jnp.dot(token_rows, up_rows, preferred_element_type=jnp.float32)
    return (jax.nn.silu(gate_part) * up_part).astype(jnp.bfloat16)


def local(
    queries,
    suffix_latent,
    cache_pool,
    holders,
    block_slots,
    prefix_len,
    hidden,
    w_value,
    w_out,
    norm_gain,
    experts,
    gate_weights,
    w_gate,
    w_up,
    w_down,
):
    rep_count = lax.axis_size("rep")
    ep_count = lax.axis_size(EP)
    rep_index = lax.axis_index("rep")
    ep_index = lax.axis_index("epo") * lax.axis_size("core") + lax.axis_index("core")
    pool_count = cache_pool.shape[1]
    block_width = cache_pool.shape[2]
    per_device = holders.shape[1] // ep_count
    per_holder = (per_device + rep_count - 1) // rep_count
    latent_width = KVR + ROPE
    mine_holders = lax.dynamic_slice_in_dim(holders, ep_index * per_device, per_device, 1)
    mine_slots = lax.dynamic_slice_in_dim(block_slots, ep_index * per_device, per_device, 1)
    position = jnp.arange(per_device, dtype=jnp.int32)
    same_holder = mine_holders[:, :, None] == mine_holders[:, None, :]
    earlier = position[None, :] < position[:, None]
    occurrence = jnp.sum((same_holder & earlier[None, :, :]).astype(jnp.int32), axis=2)
    wanted = mine_holders == rep_index
    chosen_slot = occurrence[:, :, None] == jnp.arange(per_holder, dtype=jnp.int32)[None, None, :]
    chosen_row = mine_slots[:, :, None] == jnp.arange(pool_count, dtype=jnp.int32)[None, None, :]
    selector = jnp.einsum(
        "son,soh->snh",
        (wanted[:, :, None] & chosen_slot).astype(jnp.float32),
        chosen_row.astype(jnp.float32),
        precision=lax.Precision.HIGHEST,
    )
    outgoing = jnp.dot(
        selector.reshape(rep_count * per_holder, pool_count).astype(jnp.bfloat16),
        cache_pool[0],
        preferred_element_type=jnp.float32,
    )
    outgoing = outgoing.astype(jnp.bfloat16).reshape(rep_count, per_holder, block_width)
    incoming = lax.all_to_all(outgoing, "rep", split_axis=0, concat_axis=0, tiled=True)
    own_holders = lax.dynamic_index_in_dim(mine_holders, rep_index, 0, keepdims=False)
    own_order = lax.dynamic_index_in_dim(occurrence, rep_index, 0, keepdims=False)
    source = own_holders * per_holder + own_order
    picker = (
        source[:, None] == jnp.arange(rep_count * per_holder, dtype=jnp.int32)[None, :]
    ).astype(jnp.bfloat16)
    own_blocks = jnp.dot(
        picker,
        incoming.reshape(rep_count * per_holder, block_width),
        preferred_element_type=jnp.float32,
    ).astype(jnp.bfloat16)
    core_count = lax.axis_size("core")
    outer_count = ep_count // core_count
    pre_rows = per_device * (block_width // latent_width)
    suf_rows = SUF // ep_count
    pad_rows = -(pre_rows + suf_rows) % 16
    packed = jnp.concatenate(
        [
            own_blocks.reshape(pre_rows, latent_width),
            suffix_latent.reshape(suf_rows, latent_width),
            jnp.zeros((pad_rows, latent_width), own_blocks.dtype),
        ],
        axis=0,
    )
    row_count = packed.shape[0]
    chip_keys = lax.all_gather(packed[None], "epo", axis=0, tiled=True)
    hidden_width, width = w_down.shape[1], w_down.shape[2]
    chunk = width // rep_count
    down_cols = w_down[0].reshape(hidden_width, rep_count, chunk)
    down_cols = jnp.transpose(down_cols, (1, 0, 2))
    down_cols = lax.all_to_all(down_cols, "rep", 0, 0, tiled=True)
    chip_keys, down_cols = lax.optimization_barrier((chip_keys, down_cols))
    chip_keys = jnp.broadcast_to(chip_keys[None], (core_count,) + chip_keys.shape)
    all_keys = lax.all_to_all(chip_keys, "core", 0, 0, tiled=True)
    keys = all_keys.reshape(-1, latent_width)
    core_of = lax.broadcasted_iota(jnp.int32, all_keys.shape[:3], 0)
    outer_of = lax.broadcasted_iota(jnp.int32, all_keys.shape[:3], 1)
    row_of = lax.broadcasted_iota(jnp.int32, all_keys.shape[:3], 2)
    device_of = (outer_of * core_count + core_of).reshape(-1)
    row_of = row_of.reshape(-1)
    is_prefix = (row_of < pre_rows) & (device_of * pre_rows + row_of < prefix_len[0])
    suffix_pos = device_of * suf_rows + row_of - pre_rows
    is_suffix = (row_of >= pre_rows) & (row_of < pre_rows + suf_rows)
    token_pos = jnp.arange(SUF, dtype=jnp.int32)
    visible = is_prefix[None, :] | (is_suffix[None, :] & (suffix_pos[None, :] <= token_pos[:, None]))
    query_rows = queries[0].reshape(SUF, -1, latent_width)
    scores = (
        jnp.einsum("thc,kc->htk", query_rows, keys, preferred_element_type=jnp.float32)
        * score_scale
    )
    scores = jnp.where(visible[None, :, :], scores, -1e30)
    highest = jnp.max(scores, axis=2)
    exps = jnp.exp(scores - highest[:, :, None])
    denominator = jnp.sum(exps, axis=2)
    latent = jnp.einsum(
        "htk,kc->thc",
        exps.astype(jnp.bfloat16),
        keys[:, :KVR],
        preferred_element_type=jnp.float32,
    )
    latent = (latent / jnp.transpose(denominator)[:, :, None]).astype(jnp.bfloat16)
    head_values = jnp.einsum(
        "thc,hcv->thv", latent, w_value, preferred_element_type=jnp.float32
    ).astype(jnp.bfloat16)
    head_values = head_values.reshape(outer_count, core_count, suf_rows, -1)
    head_values = jnp.transpose(head_values, (1, 0, 2, 3)).reshape(SUF, -1)
    partial = jnp.dot(head_values, w_out, preferred_element_type=jnp.float32)
    partial = partial.reshape(core_count, SUF // core_count, -1)
    partial = jnp.sum(lax.all_to_all(partial, "core", 0, 0, tiled=True), axis=0)
    partial = partial.reshape(outer_count, 16, -1).astype(jnp.bfloat16)
    attention = jnp.sum(
        lax.all_to_all(partial, "epo", 0, 0, tiled=True).astype(jnp.float32), axis=0
    )
    attention = attention.reshape(suf_rows, -1)
    residual = hidden[0].astype(jnp.float32) + attention
    scale_rows = lax.rsqrt(jnp.mean(residual * residual, axis=1, keepdims=True) + norm_eps)
    normed = (residual * scale_rows * norm_gain.astype(jnp.float32)).astype(jnp.bfloat16)
    tok_count = hidden.shape[1]
    chosen = experts[0]
    top_count = chosen.shape[1]
    expert_count = ep_count * w_gate.shape[0]
    capacity = min(tok_count, 2 * max(1, tok_count * top_count // expert_count))
    slot_count = expert_count * capacity
    flat_choice = chosen.reshape(-1)
    hits = (flat_choice[:, None] == jnp.arange(expert_count, dtype=jnp.int32)[None, :]).astype(
        jnp.int32
    )
    rank = jnp.sum((jnp.cumsum(hits, axis=0) - hits) * hits, axis=1)
    slot_id = flat_choice * capacity + rank
    slot_hot = (slot_id[:, None] == jnp.arange(slot_count, dtype=jnp.int32)[None, :]).astype(
        jnp.float32
    )
    owner = jnp.arange(flat_choice.shape[0], dtype=jnp.int32) // top_count
    token_hot = (owner[:, None] == jnp.arange(tok_count, dtype=jnp.int32)[None, :]).astype(
        jnp.float32
    )
    placing = jnp.dot(jnp.transpose(slot_hot), token_hot, precision=lax.Precision.HIGHEST)
    weighted_hot = token_hot * gate_weights[0].astype(jnp.float32).reshape(-1)[:, None]
    combine = jnp.dot(jnp.transpose(weighted_hot), slot_hot, precision=lax.Precision.HIGHEST)
    grouped = jnp.dot(
        placing.astype(jnp.bfloat16), normed, preferred_element_type=jnp.float32
    ).astype(jnp.bfloat16)
    width = grouped.shape[1]
    spread = jnp.broadcast_to(grouped.reshape(1, expert_count, 16, -1), (rep_count, expert_count, 16, width * capacity // 16))
    spread = spread.reshape(rep_count * expert_count, 16, -1)
    batch = lax.all_to_all(spread, ("rep",) + EP, split_axis=0, concat_axis=0, tiled=True)
    batch = batch.reshape(rep_count, slot_count, width)
    units = expert_units(batch.reshape(-1, width), w_gate[0], w_up[0])
    hidden_width = units.shape[1]
    unit_copies = jnp.broadcast_to(units[None], (rep_count,) + units.shape)
    units_all = lax.all_to_all(unit_copies, "rep", 0, 0, tiled=True)
    pieces = jnp.einsum("rnk,rkc->rnc", units_all, down_cols, preferred_element_type=jnp.float32)
    out_cols = jnp.sum(pieces.astype(jnp.bfloat16).astype(jnp.float32), axis=0)
    out_cols = out_cols.astype(jnp.bfloat16)
    out_cols = out_cols.reshape(rep_count, slot_count, chunk)
    back = lax.all_to_all(out_cols, "rep", 0, 0, tiled=True)
    back = jnp.transpose(back, (1, 0, 2)).reshape(expert_count, capacity * rep_count, chunk)
    served = lax.all_to_all(back, EP, split_axis=0, concat_axis=0, tiled=True)
    mixture = jnp.dot(
        combine, served.reshape(slot_count, width).astype(jnp.float32), precision=lax.Precision.HIGHEST
    )
    return (residual + mixture)[None]


def solution(mesh):
    rep_n, ep_n = mesh.devices.shape
    fine = Mesh(mesh.devices.reshape(rep_n, ep_n // 2, 2), ("rep", "epo", "core"))
    return jax.shard_map(
        local,
        mesh=fine,
        in_specs=(
            P("rep", None, EP),
            P("rep", EP),
            P("rep", EP, None),
            P(),
            P(),
            P("rep"),
            P("rep", EP, None),
            P(EP, None, None),
            P(EP, None),
            P(),
            P("rep", EP, None),
            P("rep", EP, None),
            P(EP, None, "rep"),
            P(EP, None, "rep"),
            P(EP, "rep", None),
        ),
        out_specs=P("rep", EP, None),
        check_vma=False,
    )
```

```python
import jax
import jax.numpy as jnp
from jax import lax
from jax.sharding import Mesh, PartitionSpec as P

KVR = 512
ROPE = 64
SUF = 128
EP = ("epo", "core")


score_scale = 0.07216878364870323
norm_eps = 1e-06


def expert_units(token_rows, gate_rows, up_rows):
    gate_part = jnp.dot(token_rows, gate_rows, preferred_element_type=jnp.float32)
    up_part = jnp.dot(token_rows, up_rows, preferred_element_type=jnp.float32)
    return (jax.nn.silu(gate_part) * up_part).astype(jnp.bfloat16)


def local(
    queries,
    suffix_latent,
    cache_pool,
    holders,
    block_slots,
    prefix_len,
    hidden,
    w_value,
    w_out,
    norm_gain,
    experts,
    gate_weights,
    w_gate,
    w_up,
    w_down,
):
    rep_count = lax.axis_size("rep")
    ep_count = lax.axis_size(EP)
    rep_index = lax.axis_index("rep")
    ep_index = lax.axis_index("epo") * lax.axis_size("core") + lax.axis_index("core")
    pool_count = cache_pool.shape[1]
    block_width = cache_pool.shape[2]
    per_device = holders.shape[1] // ep_count
    per_holder = (per_device + rep_count - 1) // rep_count
    latent_width = KVR + ROPE
    mine_holders = lax.dynamic_slice_in_dim(holders, ep_index * per_device, per_device, 1)
    mine_slots = lax.dynamic_slice_in_dim(block_slots, ep_index * per_device, per_device, 1)
    position = jnp.arange(per_device, dtype=jnp.int32)
    same_holder = mine_holders[:, :, None] == mine_holders[:, None, :]
    earlier = position[None, :] < position[:, None]
    occurrence = jnp.sum((same_holder & earlier[None, :, :]).astype(jnp.int32), axis=2)
    wanted = mine_holders == rep_index
    chosen_slot = occurrence[:, :, None] == jnp.arange(per_holder, dtype=jnp.int32)[None, None, :]
    chosen_row = mine_slots[:, :, None] == jnp.arange(pool_count, dtype=jnp.int32)[None, None, :]
    selector = jnp.einsum(
        "son,soh->snh",
        (wanted[:, :, None] & chosen_slot).astype(jnp.float32),
        chosen_row.astype(jnp.float32),
        precision=lax.Precision.HIGHEST,
    )
    outgoing = jnp.dot(
        selector.reshape(rep_count * per_holder, pool_count).astype(jnp.bfloat16),
        cache_pool[0],
        preferred_element_type=jnp.float32,
    )
    outgoing = outgoing.astype(jnp.bfloat16).reshape(rep_count, per_holder, block_width)
    incoming = lax.all_to_all(outgoing, "rep", split_axis=0, concat_axis=0, tiled=True)
    own_holders = lax.dynamic_index_in_dim(mine_holders, rep_index, 0, keepdims=False)
    own_order = lax.dynamic_index_in_dim(occurrence, rep_index, 0, keepdims=False)
    source = own_holders * per_holder + own_order
    picker = (
        source[:, None] == jnp.arange(rep_count * per_holder, dtype=jnp.int32)[None, :]
    ).astype(jnp.bfloat16)
    own_blocks = jnp.dot(
        picker,
        incoming.reshape(rep_count * per_holder, block_width),
        preferred_element_type=jnp.float32,
    ).astype(jnp.bfloat16)
    core_count = lax.axis_size("core")
    outer_count = ep_count // core_count
    pre_rows = per_device * (block_width // latent_width)
    suf_rows = SUF // ep_count
    pad_rows = -(pre_rows + suf_rows) % 16
    packed = jnp.concatenate(
        [
            own_blocks.reshape(pre_rows, latent_width),
            suffix_latent.reshape(suf_rows, latent_width),
            jnp.zeros((pad_rows, latent_width), own_blocks.dtype),
        ],
        axis=0,
    )
    row_count = packed.shape[0]
    chip_keys = lax.all_gather(packed[None], EP, axis=0, tiled=True)
    hidden_width, width = w_down.shape[1], w_down.shape[2]
    chunk = width // rep_count
    down_cols = w_down[0].reshape(hidden_width, rep_count, chunk)
    down_cols = jnp.transpose(down_cols, (1, 0, 2))
    down_cols = lax.all_to_all(down_cols, "rep", 0, 0, tiled=True)
    chip_keys, down_cols = lax.optimization_barrier((chip_keys, down_cols))
    keys = chip_keys.reshape(-1, latent_width)
    device_of = lax.broadcasted_iota(jnp.int32, chip_keys.shape[:2], 0).reshape(-1)
    row_of = lax.broadcasted_iota(jnp.int32, chip_keys.shape[:2], 1).reshape(-1)
    is_prefix = (row_of < pre_rows) & (device_of * pre_rows + row_of < prefix_len[0])
    suffix_pos = device_of * suf_rows + row_of - pre_rows
    is_suffix = (row_of >= pre_rows) & (row_of < pre_rows + suf_rows)
    token_pos = jnp.arange(SUF, dtype=jnp.int32)
    visible = is_prefix[None, :] | (is_suffix[None, :] & (suffix_pos[None, :] <= token_pos[:, None]))
    query_rows = queries[0].reshape(SUF, -1, latent_width)
    scores = (
        jnp.einsum("thc,kc->htk", query_rows, keys, preferred_element_type=jnp.float32)
        * score_scale
    )
    scores = jnp.where(visible[None, :, :], scores, -1e30)
    highest = jnp.max(scores, axis=2)
    exps = jnp.exp(scores - highest[:, :, None])
    denominator = jnp.sum(exps, axis=2)
    latent = jnp.einsum(
        "htk,kc->thc",
        exps.astype(jnp.bfloat16),
        keys[:, :KVR],
        preferred_element_type=jnp.float32,
    )
    latent = (latent / jnp.transpose(denominator)[:, :, None]).astype(jnp.bfloat16)
    head_values = jnp.einsum(
        "thc,hcv->thv", latent, w_value, preferred_element_type=jnp.float32
    ).astype(jnp.bfloat16)
    head_values = head_values.reshape(outer_count, core_count, suf_rows, -1)
    head_values = jnp.transpose(head_values, (1, 0, 2, 3)).reshape(SUF, -1)
    partial = jnp.dot(head_values, w_out, preferred_element_type=jnp.float32)
    partial = partial.reshape(core_count, SUF // core_count, -1)
    partial = jnp.sum(lax.all_to_all(partial, "core", 0, 0, tiled=True), axis=0)
    partial = partial.reshape(outer_count, 16, -1).astype(jnp.bfloat16)
    attention = jnp.sum(
        lax.all_to_all(partial, "epo", 0, 0, tiled=True).astype(jnp.float32), axis=0
    )
    attention = attention.reshape(suf_rows, -1)
    residual = hidden[0].astype(jnp.float32) + attention
    scale_rows = lax.rsqrt(jnp.mean(residual * residual, axis=1, keepdims=True) + norm_eps)
    normed = (residual * scale_rows * norm_gain.astype(jnp.float32)).astype(jnp.bfloat16)
    tok_count = hidden.shape[1]
    chosen = experts[0]
    top_count = chosen.shape[1]
    expert_count = ep_count * w_gate.shape[0]
    capacity = min(tok_count, 2 * max(1, tok_count * top_count // expert_count))
    slot_count = expert_count * capacity
    flat_choice = chosen.reshape(-1)
    hits = (flat_choice[:, None] == jnp.arange(expert_count, dtype=jnp.int32)[None, :]).astype(
        jnp.int32
    )
    rank = jnp.sum((jnp.cumsum(hits, axis=0) - hits) * hits, axis=1)
    slot_id = flat_choice * capacity + rank
    slot_hot = (slot_id[:, None] == jnp.arange(slot_count, dtype=jnp.int32)[None, :]).astype(
        jnp.float32
    )
    owner = jnp.arange(flat_choice.shape[0], dtype=jnp.int32) // top_count
    token_hot = (owner[:, None] == jnp.arange(tok_count, dtype=jnp.int32)[None, :]).astype(
        jnp.float32
    )
    placing = jnp.dot(jnp.transpose(slot_hot), token_hot, precision=lax.Precision.HIGHEST)
    weighted_hot = token_hot * gate_weights[0].astype(jnp.float32).reshape(-1)[:, None]
    combine = jnp.dot(jnp.transpose(weighted_hot), slot_hot, precision=lax.Precision.HIGHEST)
    grouped = jnp.dot(
        placing.astype(jnp.bfloat16), normed, preferred_element_type=jnp.float32
    ).astype(jnp.bfloat16)
    width = grouped.shape[1]
    grouped = grouped.reshape(expert_count, 16, -1)
    mine = lax.all_to_all(grouped, EP, split_axis=0, concat_axis=0, tiled=True)
    mine = mine.reshape(slot_count, width)
    copies = jnp.broadcast_to(mine[None], (rep_count,) + mine.shape)
    batch = lax.all_to_all(copies, "rep", split_axis=0, concat_axis=0, tiled=True)
    units = expert_units(batch.reshape(-1, width), w_gate[0], w_up[0])
    hidden_width = units.shape[1]
    unit_copies = jnp.broadcast_to(units[None], (rep_count,) + units.shape)
    units_all = lax.all_to_all(unit_copies, "rep", 0, 0, tiled=True)
    pieces = jnp.einsum("rnk,rkc->rnc", units_all, down_cols, preferred_element_type=jnp.float32)
    out_cols = jnp.sum(pieces.astype(jnp.bfloat16).astype(jnp.float32), axis=0)
    out_cols = out_cols.astype(jnp.bfloat16)
    out_cols = out_cols.reshape(rep_count, slot_count, chunk)
    back = lax.all_to_all(out_cols, "rep", 0, 0, tiled=True)
    back = jnp.transpose(back, (1, 0, 2)).reshape(expert_count, capacity * rep_count, chunk)
    served = lax.all_to_all(back, EP, split_axis=0, concat_axis=0, tiled=True)
    mixture = jnp.dot(
        combine, served.reshape(slot_count, width).astype(jnp.float32), precision=lax.Precision.HIGHEST
    )
    return (residual + mixture)[None]


def solution(mesh):
    rep_n, ep_n = mesh.devices.shape
    fine = Mesh(mesh.devices.reshape(rep_n, ep_n // 2, 2), ("rep", "epo", "core"))
    return jax.shard_map(
        local,
        mesh=fine,
        in_specs=(
            P("rep", None, EP),
            P("rep", EP),
            P("rep", EP, None),
            P(),
            P(),
            P("rep"),
            P("rep", EP, None),
            P(EP, None, None),
            P(EP, None),
            P(),
            P("rep", EP, None),
            P("rep", EP, None),
            P(EP, None, "rep"),
            P(EP, None, "rep"),
            P(EP, "rep", None),
        ),
        out_specs=P("rep", EP, None),
        check_vma=False,
    )
```

```python
import jax
import jax.numpy as jnp
from jax import lax
from jax.sharding import Mesh, PartitionSpec as P

KVR = 512
ROPE = 64
SUF = 128
EP = ("epo", "core")


score_scale = 0.07216878364870323
norm_eps = 1e-06


def expert_units(token_rows, gate_rows, up_rows):
    gate_part = jnp.dot(token_rows, gate_rows, preferred_element_type=jnp.float32)
    up_part = jnp.dot(token_rows, up_rows, preferred_element_type=jnp.float32)
    return (jax.nn.silu(gate_part) * up_part).astype(jnp.bfloat16)


def local(
    queries,
    suffix_latent,
    cache_pool,
    holders,
    block_slots,
    prefix_len,
    hidden,
    w_value,
    w_out,
    norm_gain,
    experts,
    gate_weights,
    w_gate,
    w_up,
    w_down,
):
    rep_count = lax.axis_size("rep")
    ep_count = lax.axis_size(EP)
    rep_index = lax.axis_index("rep")
    ep_index = lax.axis_index("epo") * lax.axis_size("core") + lax.axis_index("core")
    pool_count = cache_pool.shape[1]
    block_width = cache_pool.shape[2]
    per_device = holders.shape[1] // ep_count
    per_holder = (per_device + rep_count - 1) // rep_count
    latent_width = KVR + ROPE
    mine_holders = lax.dynamic_slice_in_dim(holders, ep_index * per_device, per_device, 1)
    mine_slots = lax.dynamic_slice_in_dim(block_slots, ep_index * per_device, per_device, 1)
    position = jnp.arange(per_device, dtype=jnp.int32)
    same_holder = mine_holders[:, :, None] == mine_holders[:, None, :]
    earlier = position[None, :] < position[:, None]
    occurrence = jnp.sum((same_holder & earlier[None, :, :]).astype(jnp.int32), axis=2)
    wanted = mine_holders == rep_index
    chosen_slot = occurrence[:, :, None] == jnp.arange(per_holder, dtype=jnp.int32)[None, None, :]
    chosen_row = mine_slots[:, :, None] == jnp.arange(pool_count, dtype=jnp.int32)[None, None, :]
    selector = jnp.einsum(
        "son,soh->snh",
        (wanted[:, :, None] & chosen_slot).astype(jnp.float32),
        chosen_row.astype(jnp.float32),
        precision=lax.Precision.HIGHEST,
    )
    outgoing = jnp.dot(
        selector.reshape(rep_count * per_holder, pool_count).astype(jnp.bfloat16),
        cache_pool[0],
        preferred_element_type=jnp.float32,
    )
    outgoing = outgoing.astype(jnp.bfloat16).reshape(rep_count, per_holder, block_width)
    incoming = lax.all_to_all(outgoing, "rep", split_axis=0, concat_axis=0, tiled=True)
    own_holders = lax.dynamic_index_in_dim(mine_holders, rep_index, 0, keepdims=False)
    own_order = lax.dynamic_index_in_dim(occurrence, rep_index, 0, keepdims=False)
    source = own_holders * per_holder + own_order
    picker = (
        source[:, None] == jnp.arange(rep_count * per_holder, dtype=jnp.int32)[None, :]
    ).astype(jnp.bfloat16)
    own_blocks = jnp.dot(
        picker,
        incoming.reshape(rep_count * per_holder, block_width),
        preferred_element_type=jnp.float32,
    ).astype(jnp.bfloat16)
    core_count = lax.axis_size("core")
    outer_count = ep_count // core_count
    pre_rows = per_device * (block_width // latent_width)
    suf_rows = SUF // ep_count
    pad_rows = -(pre_rows + suf_rows) % 16
    packed = jnp.concatenate(
        [
            own_blocks.reshape(pre_rows, latent_width),
            suffix_latent.reshape(suf_rows, latent_width),
            jnp.zeros((pad_rows, latent_width), own_blocks.dtype),
        ],
        axis=0,
    )
    row_count = packed.shape[0]
    chip_keys = lax.all_gather(packed[None], EP, axis=0, tiled=True)
    hidden_width, width = w_down.shape[1], w_down.shape[2]
    chunk = width // rep_count
    down_cols = w_down[0].reshape(hidden_width, rep_count, chunk)
    down_cols = jnp.transpose(down_cols, (1, 0, 2))
    down_cols = lax.all_to_all(down_cols, "rep", 0, 0, tiled=True)
    gate_rows = lax.all_to_all(w_gate[0].reshape(rep_count, chunk, hidden_width), "rep", 0, 0, tiled=True)
    up_rows = lax.all_to_all(w_up[0].reshape(rep_count, chunk, hidden_width), "rep", 0, 0, tiled=True)
    chip_keys, down_cols, gate_rows, up_rows = lax.optimization_barrier(
        (chip_keys, down_cols, gate_rows, up_rows)
    )
    keys = chip_keys.reshape(-1, latent_width)
    device_of = lax.broadcasted_iota(jnp.int32, chip_keys.shape[:2], 0).reshape(-1)
    row_of = lax.broadcasted_iota(jnp.int32, chip_keys.shape[:2], 1).reshape(-1)
    is_prefix = (row_of < pre_rows) & (device_of * pre_rows + row_of < prefix_len[0])
    suffix_pos = device_of * suf_rows + row_of - pre_rows
    is_suffix = (row_of >= pre_rows) & (row_of < pre_rows + suf_rows)
    token_pos = jnp.arange(SUF, dtype=jnp.int32)
    visible = is_prefix[None, :] | (is_suffix[None, :] & (suffix_pos[None, :] <= token_pos[:, None]))
    query_rows = queries[0].reshape(SUF, -1, latent_width)
    scores = (
        jnp.einsum("thc,kc->htk", query_rows, keys, preferred_element_type=jnp.float32)
        * score_scale
    )
    scores = jnp.where(visible[None, :, :], scores, -1e30)
    highest = jnp.max(scores, axis=2)
    exps = jnp.exp(scores - highest[:, :, None])
    denominator = jnp.sum(exps, axis=2)
    latent = jnp.einsum(
        "htk,kc->thc",
        exps.astype(jnp.bfloat16),
        keys[:, :KVR],
        preferred_element_type=jnp.float32,
    )
    latent = (latent / jnp.transpose(denominator)[:, :, None]).astype(jnp.bfloat16)
    head_values = jnp.einsum(
        "thc,hcv->thv", latent, w_value, preferred_element_type=jnp.float32
    ).astype(jnp.bfloat16)
    head_values = head_values.reshape(outer_count, core_count, suf_rows, -1)
    head_values = jnp.transpose(head_values, (1, 0, 2, 3)).reshape(SUF, -1)
    partial = jnp.dot(head_values, w_out, preferred_element_type=jnp.float32)
    partial = partial.reshape(core_count, SUF // core_count, -1)
    partial = jnp.sum(lax.all_to_all(partial, "core", 0, 0, tiled=True), axis=0)
    partial = partial.reshape(outer_count, 16, -1).astype(jnp.bfloat16)
    attention = jnp.sum(
        lax.all_to_all(partial, "epo", 0, 0, tiled=True).astype(jnp.float32), axis=0
    )
    attention = attention.reshape(suf_rows, -1)
    residual = hidden[0].astype(jnp.float32) + attention
    scale_rows = lax.rsqrt(jnp.mean(residual * residual, axis=1, keepdims=True) + norm_eps)
    normed = (residual * scale_rows * norm_gain.astype(jnp.float32)).astype(jnp.bfloat16)
    tok_count = hidden.shape[1]
    chosen = experts[0]
    top_count = chosen.shape[1]
    expert_count = ep_count * w_gate.shape[0]
    capacity = min(tok_count, 2 * max(1, tok_count * top_count // expert_count))
    slot_count = expert_count * capacity
    flat_choice = chosen.reshape(-1)
    hits = (flat_choice[:, None] == jnp.arange(expert_count, dtype=jnp.int32)[None, :]).astype(
        jnp.int32
    )
    rank = jnp.sum((jnp.cumsum(hits, axis=0) - hits) * hits, axis=1)
    slot_id = flat_choice * capacity + rank
    slot_hot = (slot_id[:, None] == jnp.arange(slot_count, dtype=jnp.int32)[None, :]).astype(
        jnp.float32
    )
    owner = jnp.arange(flat_choice.shape[0], dtype=jnp.int32) // top_count
    token_hot = (owner[:, None] == jnp.arange(tok_count, dtype=jnp.int32)[None, :]).astype(
        jnp.float32
    )
    placing = jnp.dot(jnp.transpose(slot_hot), token_hot, precision=lax.Precision.HIGHEST)
    weighted_hot = token_hot * gate_weights[0].astype(jnp.float32).reshape(-1)[:, None]
    combine = jnp.dot(jnp.transpose(weighted_hot), slot_hot, precision=lax.Precision.HIGHEST)
    grouped = jnp.dot(
        placing.astype(jnp.bfloat16), normed, preferred_element_type=jnp.float32
    ).astype(jnp.bfloat16)
    width = grouped.shape[1]
    grouped = grouped.reshape(expert_count, 16, -1)
    mine = lax.all_to_all(grouped, EP, split_axis=0, concat_axis=0, tiled=True)
    mine = mine.reshape(slot_count, rep_count, chunk)
    mine = jnp.transpose(mine, (1, 0, 2))
    columns = lax.all_to_all(mine, "rep", 0, 0, tiled=True).reshape(-1, chunk)
    gate_part = jnp.einsum("nd,rdk->rnk", columns, gate_rows, preferred_element_type=jnp.float32)
    up_part = jnp.einsum("nd,rdk->rnk", columns, up_rows, preferred_element_type=jnp.float32)
    parts = jnp.concatenate([gate_part, up_part], axis=2).astype(jnp.bfloat16)
    parts = lax.all_to_all(parts, "rep", 0, 0, tiled=True)
    sums = jnp.sum(parts.astype(jnp.float32), axis=0)
    gate_sum, up_sum = sums[:, :hidden_width], sums[:, hidden_width:]
    units = (jax.nn.silu(gate_sum) * up_sum).astype(jnp.bfloat16)
    hidden_width = units.shape[1]
    unit_copies = jnp.broadcast_to(units[None], (rep_count,) + units.shape)
    units_all = lax.all_to_all(unit_copies, "rep", 0, 0, tiled=True)
    pieces = jnp.einsum("rnk,rkc->rnc", units_all, down_cols, preferred_element_type=jnp.float32)
    out_cols = jnp.sum(pieces.astype(jnp.bfloat16).astype(jnp.float32), axis=0)
    out_cols = out_cols.astype(jnp.bfloat16)
    out_cols = out_cols.reshape(rep_count, slot_count, chunk)
    back = lax.all_to_all(out_cols, "rep", 0, 0, tiled=True)
    back = jnp.transpose(back, (1, 0, 2)).reshape(expert_count, capacity * rep_count, chunk)
    served = lax.all_to_all(back, EP, split_axis=0, concat_axis=0, tiled=True)
    mixture = jnp.dot(
        combine, served.reshape(slot_count, width).astype(jnp.float32), precision=lax.Precision.HIGHEST
    )
    return (residual + mixture)[None]


def solution(mesh):
    rep_n, ep_n = mesh.devices.shape
    fine = Mesh(mesh.devices.reshape(rep_n, ep_n // 2, 2), ("rep", "epo", "core"))
    return jax.shard_map(
        local,
        mesh=fine,
        in_specs=(
            P("rep", None, EP),
            P("rep", EP),
            P("rep", EP, None),
            P(),
            P(),
            P("rep"),
            P("rep", EP, None),
            P(EP, None, None),
            P(EP, None),
            P(),
            P("rep", EP, None),
            P("rep", EP, None),
            P(EP, None, "rep"),
            P(EP, None, "rep"),
            P(EP, "rep", None),
        ),
        out_specs=P("rep", EP, None),
        check_vma=False,
    )
```

```python
import jax
import jax.numpy as jnp
from jax import lax
from jax.sharding import Mesh, PartitionSpec as P

KVR = 512
ROPE = 64
SUF = 128
EP = ("epo", "core")


score_scale = 0.07216878364870323
norm_eps = 1e-06


def expert_units(token_rows, gate_rows, up_rows):
    gate_part = jnp.dot(token_rows, gate_rows, preferred_element_type=jnp.float32)
    up_part = jnp.dot(token_rows, up_rows, preferred_element_type=jnp.float32)
    return (jax.nn.silu(gate_part) * up_part).astype(jnp.bfloat16)


def local(
    queries,
    suffix_latent,
    cache_pool,
    holders,
    block_slots,
    prefix_len,
    hidden,
    w_value,
    w_out,
    norm_gain,
    experts,
    gate_weights,
    w_gate,
    w_up,
    w_down,
):
    rep_count = lax.axis_size("rep")
    ep_count = lax.axis_size(EP)
    rep_index = lax.axis_index("rep")
    ep_index = lax.axis_index("epo") * lax.axis_size("core") + lax.axis_index("core")
    pool_count = cache_pool.shape[1]
    block_width = cache_pool.shape[2]
    per_device = holders.shape[1] // ep_count
    per_holder = (per_device + rep_count - 1) // rep_count
    latent_width = KVR + ROPE
    mine_holders = lax.dynamic_slice_in_dim(holders, ep_index * per_device, per_device, 1)
    mine_slots = lax.dynamic_slice_in_dim(block_slots, ep_index * per_device, per_device, 1)
    position = jnp.arange(per_device, dtype=jnp.int32)
    same_holder = mine_holders[:, :, None] == mine_holders[:, None, :]
    earlier = position[None, :] < position[:, None]
    occurrence = jnp.sum((same_holder & earlier[None, :, :]).astype(jnp.int32), axis=2)
    wanted = mine_holders == rep_index
    chosen_slot = occurrence[:, :, None] == jnp.arange(per_holder, dtype=jnp.int32)[None, None, :]
    chosen_row = mine_slots[:, :, None] == jnp.arange(pool_count, dtype=jnp.int32)[None, None, :]
    selector = jnp.einsum(
        "son,soh->snh",
        (wanted[:, :, None] & chosen_slot).astype(jnp.float32),
        chosen_row.astype(jnp.float32),
        precision=lax.Precision.HIGHEST,
    )
    outgoing = jnp.dot(
        selector.reshape(rep_count * per_holder, pool_count).astype(jnp.bfloat16),
        cache_pool[0],
        preferred_element_type=jnp.float32,
    )
    outgoing = outgoing.astype(jnp.bfloat16).reshape(rep_count, per_holder, block_width)
    incoming = lax.all_to_all(outgoing, "rep", split_axis=0, concat_axis=0, tiled=True)
    own_holders = lax.dynamic_index_in_dim(mine_holders, rep_index, 0, keepdims=False)
    own_order = lax.dynamic_index_in_dim(occurrence, rep_index, 0, keepdims=False)
    source = own_holders * per_holder + own_order
    picker = (
        source[:, None] == jnp.arange(rep_count * per_holder, dtype=jnp.int32)[None, :]
    ).astype(jnp.bfloat16)
    own_blocks = jnp.dot(
        picker,
        incoming.reshape(rep_count * per_holder, block_width),
        preferred_element_type=jnp.float32,
    ).astype(jnp.bfloat16)
    core_count = lax.axis_size("core")
    outer_count = ep_count // core_count
    pre_rows = per_device * (block_width // latent_width)
    suf_rows = SUF // ep_count
    pad_rows = -(pre_rows + suf_rows) % 16
    packed = jnp.concatenate(
        [
            own_blocks.reshape(pre_rows, latent_width),
            suffix_latent.reshape(suf_rows, latent_width),
            jnp.zeros((pad_rows, latent_width), own_blocks.dtype),
        ],
        axis=0,
    )
    row_count = packed.shape[0]
    chip_keys = lax.all_gather(packed[None], EP, axis=0, tiled=True)
    hidden_width, width = w_down.shape[1], w_down.shape[2]
    chunk = width // rep_count
    down_cols = w_down[0].reshape(hidden_width, rep_count, chunk)
    down_cols = jnp.transpose(down_cols, (1, 0, 2))
    down_cols = lax.all_to_all(down_cols, "rep", 0, 0, tiled=True)
    gate_rows = lax.all_to_all(w_gate[0].reshape(rep_count, chunk, hidden_width), "rep", 0, 0, tiled=True)
    up_rows = lax.all_to_all(w_up[0].reshape(rep_count, chunk, hidden_width), "rep", 0, 0, tiled=True)
    chip_keys, down_cols, gate_rows, up_rows = lax.optimization_barrier(
        (chip_keys, down_cols, gate_rows, up_rows)
    )
    keys = chip_keys.reshape(-1, latent_width)
    device_of = lax.broadcasted_iota(jnp.int32, chip_keys.shape[:2], 0).reshape(-1)
    row_of = lax.broadcasted_iota(jnp.int32, chip_keys.shape[:2], 1).reshape(-1)
    is_prefix = (row_of < pre_rows) & (device_of * pre_rows + row_of < prefix_len[0])
    suffix_pos = device_of * suf_rows + row_of - pre_rows
    is_suffix = (row_of >= pre_rows) & (row_of < pre_rows + suf_rows)
    token_pos = jnp.arange(SUF, dtype=jnp.int32)
    visible = is_prefix[None, :] | (is_suffix[None, :] & (suffix_pos[None, :] <= token_pos[:, None]))
    query_rows = queries[0].reshape(SUF, -1, latent_width)
    scores = (
        jnp.einsum("thc,kc->htk", query_rows, keys, preferred_element_type=jnp.float32)
        * score_scale
    )
    scores = jnp.where(visible[None, :, :], scores, -1e30)
    highest = jnp.max(scores, axis=2)
    exps = jnp.exp(scores - highest[:, :, None])
    denominator = jnp.sum(exps, axis=2)
    latent = jnp.einsum(
        "htk,kc->thc",
        exps.astype(jnp.bfloat16),
        keys[:, :KVR],
        preferred_element_type=jnp.float32,
    )
    latent = (latent / jnp.transpose(denominator)[:, :, None]).astype(jnp.bfloat16)
    head_values = jnp.einsum(
        "thc,hcv->thv", latent, w_value, preferred_element_type=jnp.float32
    ).astype(jnp.bfloat16)
    head_values = head_values.reshape(outer_count, core_count, suf_rows, -1)
    head_values = jnp.transpose(head_values, (1, 0, 2, 3)).reshape(SUF, -1)
    partial = jnp.dot(head_values, w_out, preferred_element_type=jnp.float32)
    partial = partial.reshape(core_count, SUF // core_count, -1)
    partial = jnp.sum(lax.all_to_all(partial, "core", 0, 0, tiled=True), axis=0)
    partial = partial.reshape(outer_count, 16, -1).astype(jnp.bfloat16)
    attention = jnp.sum(
        lax.all_to_all(partial, "epo", 0, 0, tiled=True).astype(jnp.float32), axis=0
    )
    attention = attention.reshape(suf_rows, -1)
    residual = hidden[0].astype(jnp.float32) + attention
    scale_rows = lax.rsqrt(jnp.mean(residual * residual, axis=1, keepdims=True) + norm_eps)
    normed = (residual * scale_rows * norm_gain.astype(jnp.float32)).astype(jnp.bfloat16)
    tok_count = hidden.shape[1]
    chosen = experts[0]
    top_count = chosen.shape[1]
    expert_count = ep_count * w_gate.shape[0]
    capacity = min(tok_count, 2 * max(1, tok_count * top_count // expert_count))
    slot_count = expert_count * capacity
    flat_choice = chosen.reshape(-1)
    hits = (flat_choice[:, None] == jnp.arange(expert_count, dtype=jnp.int32)[None, :]).astype(
        jnp.int32
    )
    rank = jnp.sum((jnp.cumsum(hits, axis=0) - hits) * hits, axis=1)
    slot_id = flat_choice * capacity + rank
    slot_hot = (slot_id[:, None] == jnp.arange(slot_count, dtype=jnp.int32)[None, :]).astype(
        jnp.float32
    )
    owner = jnp.arange(flat_choice.shape[0], dtype=jnp.int32) // top_count
    token_hot = (owner[:, None] == jnp.arange(tok_count, dtype=jnp.int32)[None, :]).astype(
        jnp.float32
    )
    placing = jnp.dot(jnp.transpose(slot_hot), token_hot, precision=lax.Precision.HIGHEST)
    weighted_hot = token_hot * gate_weights[0].astype(jnp.float32).reshape(-1)[:, None]
    combine = jnp.dot(jnp.transpose(weighted_hot), slot_hot, precision=lax.Precision.HIGHEST)
    grouped = jnp.dot(
        placing.astype(jnp.bfloat16), normed, preferred_element_type=jnp.float32
    ).astype(jnp.bfloat16)
    width = grouped.shape[1]
    spread = grouped.reshape(expert_count, capacity, rep_count, chunk)
    spread = jnp.transpose(spread, (2, 0, 1, 3)).reshape(rep_count * expert_count, capacity, chunk)
    columns = lax.all_to_all(spread, ("rep",) + EP, 0, 0, tiled=True).reshape(-1, chunk)
    gate_part = jnp.einsum("nd,rdk->rnk", columns, gate_rows, preferred_element_type=jnp.float32)
    up_part = jnp.einsum("nd,rdk->rnk", columns, up_rows, preferred_element_type=jnp.float32)
    parts = jnp.concatenate([gate_part, up_part], axis=2).astype(jnp.bfloat16)
    parts = lax.all_to_all(parts, "rep", 0, 0, tiled=True)
    sums = jnp.sum(parts.astype(jnp.float32), axis=0)
    gate_sum, up_sum = sums[:, :hidden_width], sums[:, hidden_width:]
    units = (jax.nn.silu(gate_sum) * up_sum).astype(jnp.bfloat16)
    hidden_width = units.shape[1]
    unit_copies = jnp.broadcast_to(units[None], (rep_count,) + units.shape)
    units_all = lax.all_to_all(unit_copies, "rep", 0, 0, tiled=True)
    pieces = jnp.einsum("rnk,rkc->rnc", units_all, down_cols, preferred_element_type=jnp.float32)
    out_cols = jnp.sum(pieces.astype(jnp.bfloat16).astype(jnp.float32), axis=0)
    out_cols = out_cols.astype(jnp.bfloat16)
    out_cols = out_cols.reshape(rep_count, slot_count, chunk)
    back = lax.all_to_all(out_cols, "rep", 0, 0, tiled=True)
    back = jnp.transpose(back, (1, 0, 2)).reshape(expert_count, capacity * rep_count, chunk)
    served = lax.all_to_all(back, EP, split_axis=0, concat_axis=0, tiled=True)
    mixture = jnp.dot(
        combine, served.reshape(slot_count, width).astype(jnp.float32), precision=lax.Precision.HIGHEST
    )
    return (residual + mixture)[None]


def solution(mesh):
    rep_n, ep_n = mesh.devices.shape
    fine = Mesh(mesh.devices.reshape(rep_n, ep_n // 2, 2), ("rep", "epo", "core"))
    return jax.shard_map(
        local,
        mesh=fine,
        in_specs=(
            P("rep", None, EP),
            P("rep", EP),
            P("rep", EP, None),
            P(),
            P(),
            P("rep"),
            P("rep", EP, None),
            P(EP, None, None),
            P(EP, None),
            P(),
            P("rep", EP, None),
            P("rep", EP, None),
            P(EP, None, "rep"),
            P(EP, None, "rep"),
            P(EP, "rep", None),
        ),
        out_specs=P("rep", EP, None),
        check_vma=False,
    )
```

```python
import jax
import jax.numpy as jnp
from jax import lax
from jax.sharding import Mesh, PartitionSpec as P

KVR = 512
ROPE = 64
SUF = 128
EP = ("epo", "core")


score_scale = 0.07216878364870323
norm_eps = 1e-06


def expert_units(token_rows, gate_rows, up_rows):
    gate_part = jnp.dot(token_rows, gate_rows, preferred_element_type=jnp.float32)
    up_part = jnp.dot(token_rows, up_rows, preferred_element_type=jnp.float32)
    return (jax.nn.silu(gate_part) * up_part).astype(jnp.bfloat16)


def local(
    queries,
    suffix_latent,
    cache_pool,
    holders,
    block_slots,
    prefix_len,
    hidden,
    w_value,
    w_out,
    norm_gain,
    experts,
    gate_weights,
    w_gate,
    w_up,
    w_down,
):
    rep_count = lax.axis_size("rep")
    ep_count = lax.axis_size(EP)
    rep_index = lax.axis_index("rep")
    ep_index = lax.axis_index("epo") * lax.axis_size("core") + lax.axis_index("core")
    pool_count = cache_pool.shape[1]
    block_width = cache_pool.shape[2]
    per_device = holders.shape[1] // ep_count
    per_holder = (per_device + rep_count - 1) // rep_count
    latent_width = KVR + ROPE
    mine_holders = lax.dynamic_slice_in_dim(holders, ep_index * per_device, per_device, 1)
    mine_slots = lax.dynamic_slice_in_dim(block_slots, ep_index * per_device, per_device, 1)
    position = jnp.arange(per_device, dtype=jnp.int32)
    same_holder = mine_holders[:, :, None] == mine_holders[:, None, :]
    earlier = position[None, :] < position[:, None]
    occurrence = jnp.sum((same_holder & earlier[None, :, :]).astype(jnp.int32), axis=2)
    wanted = mine_holders == rep_index
    chosen_slot = occurrence[:, :, None] == jnp.arange(per_holder, dtype=jnp.int32)[None, None, :]
    chosen_row = mine_slots[:, :, None] == jnp.arange(pool_count, dtype=jnp.int32)[None, None, :]
    selector = jnp.einsum(
        "son,soh->snh",
        (wanted[:, :, None] & chosen_slot).astype(jnp.float32),
        chosen_row.astype(jnp.float32),
        precision=lax.Precision.HIGHEST,
    )
    outgoing = jnp.dot(
        selector.reshape(rep_count * per_holder, pool_count).astype(jnp.bfloat16),
        cache_pool[0],
        preferred_element_type=jnp.float32,
    )
    outgoing = outgoing.astype(jnp.bfloat16).reshape(rep_count, per_holder, block_width)
    incoming = lax.all_to_all(outgoing, "rep", split_axis=0, concat_axis=0, tiled=True)
    own_holders = lax.dynamic_index_in_dim(mine_holders, rep_index, 0, keepdims=False)
    own_order = lax.dynamic_index_in_dim(occurrence, rep_index, 0, keepdims=False)
    source = own_holders * per_holder + own_order
    picker = (
        source[:, None] == jnp.arange(rep_count * per_holder, dtype=jnp.int32)[None, :]
    ).astype(jnp.bfloat16)
    own_blocks = jnp.dot(
        picker,
        incoming.reshape(rep_count * per_holder, block_width),
        preferred_element_type=jnp.float32,
    ).astype(jnp.bfloat16)
    core_count = lax.axis_size("core")
    outer_count = ep_count // core_count
    pre_rows = per_device * (block_width // latent_width)
    suf_rows = SUF // ep_count
    pad_rows = -(pre_rows + suf_rows) % 16
    packed = jnp.concatenate(
        [
            own_blocks.reshape(pre_rows, latent_width),
            suffix_latent.reshape(suf_rows, latent_width),
            jnp.zeros((pad_rows, latent_width), own_blocks.dtype),
        ],
        axis=0,
    )
    row_count = packed.shape[0]
    chip_keys = lax.all_gather(packed[None], EP, axis=0, tiled=True)
    hidden_width, width = w_down.shape[1], w_down.shape[2]
    chunk = width // rep_count
    down_cols = w_down[0].reshape(hidden_width, rep_count, chunk)
    down_cols = jnp.transpose(down_cols, (1, 0, 2))
    down_cols = lax.all_to_all(down_cols, "rep", 0, 0, tiled=True)
    gate_rows = lax.all_to_all(w_gate[0].reshape(rep_count, chunk, hidden_width), "rep", 0, 0, tiled=True)
    up_rows = lax.all_to_all(w_up[0].reshape(rep_count, chunk, hidden_width), "rep", 0, 0, tiled=True)
    chip_keys, down_cols, gate_rows, up_rows = lax.optimization_barrier(
        (chip_keys, down_cols, gate_rows, up_rows)
    )
    keys = chip_keys.reshape(-1, latent_width)
    device_of = lax.broadcasted_iota(jnp.int32, chip_keys.shape[:2], 0).reshape(-1)
    row_of = lax.broadcasted_iota(jnp.int32, chip_keys.shape[:2], 1).reshape(-1)
    is_prefix = (row_of < pre_rows) & (device_of * pre_rows + row_of < prefix_len[0])
    suffix_pos = device_of * suf_rows + row_of - pre_rows
    is_suffix = (row_of >= pre_rows) & (row_of < pre_rows + suf_rows)
    token_pos = jnp.arange(SUF, dtype=jnp.int32)
    visible = is_prefix[None, :] | (is_suffix[None, :] & (suffix_pos[None, :] <= token_pos[:, None]))
    query_rows = queries[0].reshape(SUF, -1, latent_width)
    scores = (
        jnp.einsum("thc,kc->htk", query_rows, keys, preferred_element_type=jnp.float32)
        * score_scale
    )
    scores = jnp.where(visible[None, :, :], scores, -1e30)
    highest = jnp.max(scores, axis=2)
    exps = jnp.exp(scores - highest[:, :, None])
    denominator = jnp.sum(exps, axis=2)
    latent = jnp.einsum(
        "htk,kc->thc",
        exps.astype(jnp.bfloat16),
        keys[:, :KVR],
        preferred_element_type=jnp.float32,
    )
    latent = (latent / jnp.transpose(denominator)[:, :, None]).astype(jnp.bfloat16)
    head_values = jnp.einsum(
        "thc,hcv->thv", latent, w_value, preferred_element_type=jnp.float32
    ).astype(jnp.bfloat16)
    head_values = head_values.reshape(outer_count, core_count, suf_rows, -1)
    head_values = jnp.transpose(head_values, (1, 0, 2, 3)).reshape(SUF, -1)
    partial = jnp.dot(head_values, w_out, preferred_element_type=jnp.float32)
    partial = partial.reshape(core_count, SUF // core_count, -1)
    partial = jnp.sum(lax.all_to_all(partial, "core", 0, 0, tiled=True), axis=0)
    partial = partial.reshape(outer_count, 16, -1).astype(jnp.bfloat16)
    attention = jnp.sum(
        lax.all_to_all(partial, "epo", 0, 0, tiled=True).astype(jnp.float32), axis=0
    )
    attention = attention.reshape(suf_rows, -1)
    residual = hidden[0].astype(jnp.float32) + attention
    scale_rows = lax.rsqrt(jnp.mean(residual * residual, axis=1, keepdims=True) + norm_eps)
    normed = (residual * scale_rows * norm_gain.astype(jnp.float32)).astype(jnp.bfloat16)
    tok_count = hidden.shape[1]
    chosen = experts[0]
    top_count = chosen.shape[1]
    expert_count = ep_count * w_gate.shape[0]
    capacity = min(tok_count, 2 * max(1, tok_count * top_count // expert_count))
    slot_count = expert_count * capacity
    flat_choice = chosen.reshape(-1)
    hits = (flat_choice[:, None] == jnp.arange(expert_count, dtype=jnp.int32)[None, :]).astype(
        jnp.int32
    )
    rank = jnp.sum((jnp.cumsum(hits, axis=0) - hits) * hits, axis=1)
    slot_id = flat_choice * capacity + rank
    slot_hot = (slot_id[:, None] == jnp.arange(slot_count, dtype=jnp.int32)[None, :]).astype(
        jnp.float32
    )
    owner = jnp.arange(flat_choice.shape[0], dtype=jnp.int32) // top_count
    token_hot = (owner[:, None] == jnp.arange(tok_count, dtype=jnp.int32)[None, :]).astype(
        jnp.float32
    )
    placing = jnp.dot(jnp.transpose(slot_hot), token_hot, precision=lax.Precision.HIGHEST)
    weighted_hot = token_hot * gate_weights[0].astype(jnp.float32).reshape(-1)[:, None]
    combine = jnp.dot(jnp.transpose(weighted_hot), slot_hot, precision=lax.Precision.HIGHEST)
    grouped = jnp.dot(
        placing.astype(jnp.bfloat16), normed, preferred_element_type=jnp.float32
    ).astype(jnp.bfloat16)
    width = grouped.shape[1]
    spread = grouped.reshape(expert_count, capacity, rep_count, chunk)
    spread = jnp.transpose(spread, (2, 0, 1, 3)).reshape(rep_count * expert_count, capacity, chunk)
    columns = lax.all_to_all(spread, ("rep",) + EP, 0, 0, tiled=True).reshape(-1, chunk)
    gate_part = jnp.einsum("nd,rdk->rnk", columns, gate_rows, preferred_element_type=jnp.float32)
    up_part = jnp.einsum("nd,rdk->rnk", columns, up_rows, preferred_element_type=jnp.float32)
    parts = jnp.concatenate([gate_part, up_part], axis=2).astype(jnp.bfloat16)
    parts = lax.all_to_all(parts, "rep", 0, 0, tiled=True)
    sums = jnp.sum(parts.astype(jnp.float32), axis=0)
    gate_sum, up_sum = sums[:, :hidden_width], sums[:, hidden_width:]
    units = (jax.nn.silu(gate_sum) * up_sum).astype(jnp.bfloat16)
    hidden_width = units.shape[1]
    unit_copies = jnp.broadcast_to(units[None], (rep_count,) + units.shape)
    units_all = lax.all_to_all(unit_copies, "rep", 0, 0, tiled=True)
    pieces = jnp.einsum("rnk,rkc->rnc", units_all, down_cols, preferred_element_type=jnp.float32)
    out_cols = jnp.sum(pieces.astype(jnp.bfloat16).astype(jnp.float32), axis=0)
    out_cols = out_cols.astype(jnp.bfloat16)
    out_cols = out_cols.reshape(rep_count * expert_count, capacity, chunk)
    back = lax.all_to_all(out_cols, ("rep",) + EP, 0, 0, tiled=True)
    back = back.reshape(rep_count, expert_count, capacity, chunk)
    served = jnp.transpose(back, (1, 2, 0, 3))
    mixture = jnp.dot(
        combine, served.reshape(slot_count, width).astype(jnp.float32), precision=lax.Precision.HIGHEST
    )
    return (residual + mixture)[None]


def solution(mesh):
    rep_n, ep_n = mesh.devices.shape
    fine = Mesh(mesh.devices.reshape(rep_n, ep_n // 2, 2), ("rep", "epo", "core"))
    return jax.shard_map(
        local,
        mesh=fine,
        in_specs=(
            P("rep", None, EP),
            P("rep", EP),
            P("rep", EP, None),
            P(),
            P(),
            P("rep"),
            P("rep", EP, None),
            P(EP, None, None),
            P(EP, None),
            P(),
            P("rep", EP, None),
            P("rep", EP, None),
            P(EP, None, "rep"),
            P(EP, None, "rep"),
            P(EP, "rep", None),
        ),
        out_specs=P("rep", EP, None),
        check_vma=False,
    )
```

```python
import jax
import jax.numpy as jnp
from jax import lax
from jax.sharding import Mesh, PartitionSpec as P

KVR = 512
ROPE = 64
SUF = 128
EP = ("epo", "core")


score_scale = 0.07216878364870323
norm_eps = 1e-06


def expert_units(token_rows, gate_rows, up_rows):
    gate_part = jnp.dot(token_rows, gate_rows, preferred_element_type=jnp.float32)
    up_part = jnp.dot(token_rows, up_rows, preferred_element_type=jnp.float32)
    return (jax.nn.silu(gate_part) * up_part).astype(jnp.bfloat16)


def local(
    queries,
    suffix_latent,
    cache_pool,
    holders,
    block_slots,
    prefix_len,
    hidden,
    w_value,
    w_out,
    norm_gain,
    experts,
    gate_weights,
    w_gate,
    w_up,
    w_down,
):
    rep_count = lax.axis_size("rep")
    ep_count = lax.axis_size(EP)
    rep_index = lax.axis_index("rep")
    ep_index = lax.axis_index("epo") * lax.axis_size("core") + lax.axis_index("core")
    pool_count = cache_pool.shape[1]
    block_width = cache_pool.shape[2]
    per_device = holders.shape[1] // ep_count
    per_holder = (per_device + rep_count - 1) // rep_count
    latent_width = KVR + ROPE
    mine_holders = lax.dynamic_slice_in_dim(holders, ep_index * per_device, per_device, 1)
    mine_slots = lax.dynamic_slice_in_dim(block_slots, ep_index * per_device, per_device, 1)
    position = jnp.arange(per_device, dtype=jnp.int32)
    same_holder = mine_holders[:, :, None] == mine_holders[:, None, :]
    earlier = position[None, :] < position[:, None]
    occurrence = jnp.sum((same_holder & earlier[None, :, :]).astype(jnp.int32), axis=2)
    wanted = mine_holders == rep_index
    chosen_slot = occurrence[:, :, None] == jnp.arange(per_holder, dtype=jnp.int32)[None, None, :]
    chosen_row = mine_slots[:, :, None] == jnp.arange(pool_count, dtype=jnp.int32)[None, None, :]
    selector = jnp.einsum(
        "son,soh->snh",
        (wanted[:, :, None] & chosen_slot).astype(jnp.float32),
        chosen_row.astype(jnp.float32),
        precision=lax.Precision.HIGHEST,
    )
    outgoing = jnp.dot(
        selector.reshape(rep_count * per_holder, pool_count).astype(jnp.bfloat16),
        cache_pool[0],
        preferred_element_type=jnp.float32,
    )
    outgoing = outgoing.astype(jnp.bfloat16).reshape(rep_count, per_holder, block_width)
    incoming = lax.all_to_all(outgoing, "rep", split_axis=0, concat_axis=0, tiled=True)
    own_holders = lax.dynamic_index_in_dim(mine_holders, rep_index, 0, keepdims=False)
    own_order = lax.dynamic_index_in_dim(occurrence, rep_index, 0, keepdims=False)
    source = own_holders * per_holder + own_order
    picker = (
        source[:, None] == jnp.arange(rep_count * per_holder, dtype=jnp.int32)[None, :]
    ).astype(jnp.bfloat16)
    own_blocks = jnp.dot(
        picker,
        incoming.reshape(rep_count * per_holder, block_width),
        preferred_element_type=jnp.float32,
    ).astype(jnp.bfloat16)
    core_count = lax.axis_size("core")
    outer_count = ep_count // core_count
    pre_rows = per_device * (block_width // latent_width)
    suf_rows = SUF // ep_count
    pad_rows = -(pre_rows + suf_rows) % 16
    packed = jnp.concatenate(
        [
            own_blocks.reshape(pre_rows, latent_width),
            suffix_latent.reshape(suf_rows, latent_width),
            jnp.zeros((pad_rows, latent_width), own_blocks.dtype),
        ],
        axis=0,
    )
    row_count = packed.shape[0]
    chip_keys = lax.all_gather(packed[None], EP, axis=0, tiled=True)
    hidden_width, width = w_down.shape[1], w_down.shape[2]
    chunk = width // rep_count
    down_cols = w_down[0].reshape(hidden_width, rep_count, chunk)
    down_cols = jnp.transpose(down_cols, (1, 0, 2))
    piece = chunk * hidden_width
    bundle = jnp.concatenate(
        [
            down_cols.reshape(rep_count, piece // 1024, 1024),
            w_gate[0].reshape(rep_count, piece // 1024, 1024),
            w_up[0].reshape(rep_count, piece // 1024, 1024),
        ],
        axis=1,
    )
    bundle = lax.all_to_all(bundle, "rep", 0, 0, tiled=True)
    rows_each = piece // 1024
    down_cols = bundle[:, :rows_each].reshape(rep_count, hidden_width, chunk)
    gate_rows = bundle[:, rows_each : 2 * rows_each].reshape(rep_count, chunk, hidden_width)
    up_rows = bundle[:, 2 * rows_each :].reshape(rep_count, chunk, hidden_width)
    chip_keys, down_cols, gate_rows, up_rows = lax.optimization_barrier(
        (chip_keys, down_cols, gate_rows, up_rows)
    )
    keys = chip_keys.reshape(-1, latent_width)
    device_of = lax.broadcasted_iota(jnp.int32, chip_keys.shape[:2], 0).reshape(-1)
    row_of = lax.broadcasted_iota(jnp.int32, chip_keys.shape[:2], 1).reshape(-1)
    is_prefix = (row_of < pre_rows) & (device_of * pre_rows + row_of < prefix_len[0])
    suffix_pos = device_of * suf_rows + row_of - pre_rows
    is_suffix = (row_of >= pre_rows) & (row_of < pre_rows + suf_rows)
    token_pos = jnp.arange(SUF, dtype=jnp.int32)
    visible = is_prefix[None, :] | (is_suffix[None, :] & (suffix_pos[None, :] <= token_pos[:, None]))
    query_rows = queries[0].reshape(SUF, -1, latent_width)
    scores = (
        jnp.einsum("thc,kc->htk", query_rows, keys, preferred_element_type=jnp.float32)
        * score_scale
    )
    scores = jnp.where(visible[None, :, :], scores, -1e30)
    highest = jnp.max(scores, axis=2)
    exps = jnp.exp(scores - highest[:, :, None])
    denominator = jnp.sum(exps, axis=2)
    latent = jnp.einsum(
        "htk,kc->thc",
        exps.astype(jnp.bfloat16),
        keys[:, :KVR],
        preferred_element_type=jnp.float32,
    )
    latent = (latent / jnp.transpose(denominator)[:, :, None]).astype(jnp.bfloat16)
    head_values = jnp.einsum(
        "thc,hcv->thv", latent, w_value, preferred_element_type=jnp.float32
    ).astype(jnp.bfloat16)
    head_values = head_values.reshape(outer_count, core_count, suf_rows, -1)
    head_values = jnp.transpose(head_values, (1, 0, 2, 3)).reshape(SUF, -1)
    partial = jnp.dot(head_values, w_out, preferred_element_type=jnp.float32)
    partial = partial.reshape(core_count, SUF // core_count, -1)
    partial = jnp.sum(lax.all_to_all(partial, "core", 0, 0, tiled=True), axis=0)
    partial = partial.reshape(outer_count, 16, -1).astype(jnp.bfloat16)
    attention = jnp.sum(
        lax.all_to_all(partial, "epo", 0, 0, tiled=True).astype(jnp.float32), axis=0
    )
    attention = attention.reshape(suf_rows, -1)
    residual = hidden[0].astype(jnp.float32) + attention
    scale_rows = lax.rsqrt(jnp.mean(residual * residual, axis=1, keepdims=True) + norm_eps)
    normed = (residual * scale_rows * norm_gain.astype(jnp.float32)).astype(jnp.bfloat16)
    tok_count = hidden.shape[1]
    chosen = experts[0]
    top_count = chosen.shape[1]
    expert_count = ep_count * w_gate.shape[0]
    capacity = min(tok_count, 2 * max(1, tok_count * top_count // expert_count))
    slot_count = expert_count * capacity
    flat_choice = chosen.reshape(-1)
    hits = (flat_choice[:, None] == jnp.arange(expert_count, dtype=jnp.int32)[None, :]).astype(
        jnp.int32
    )
    rank = jnp.sum((jnp.cumsum(hits, axis=0) - hits) * hits, axis=1)
    slot_id = flat_choice * capacity + rank
    slot_hot = (slot_id[:, None] == jnp.arange(slot_count, dtype=jnp.int32)[None, :]).astype(
        jnp.float32
    )
    owner = jnp.arange(flat_choice.shape[0], dtype=jnp.int32) // top_count
    token_hot = (owner[:, None] == jnp.arange(tok_count, dtype=jnp.int32)[None, :]).astype(
        jnp.float32
    )
    placing = jnp.dot(jnp.transpose(slot_hot), token_hot, precision=lax.Precision.HIGHEST)
    weighted_hot = token_hot * gate_weights[0].astype(jnp.float32).reshape(-1)[:, None]
    combine = jnp.dot(jnp.transpose(weighted_hot), slot_hot, precision=lax.Precision.HIGHEST)
    grouped = jnp.dot(
        placing.astype(jnp.bfloat16), normed, preferred_element_type=jnp.float32
    ).astype(jnp.bfloat16)
    width = grouped.shape[1]
    spread = grouped.reshape(expert_count, capacity, rep_count, chunk)
    spread = jnp.transpose(spread, (2, 0, 1, 3)).reshape(rep_count * expert_count, capacity, chunk)
    columns = lax.all_to_all(spread, ("rep",) + EP, 0, 0, tiled=True).reshape(-1, chunk)
    gate_part = jnp.einsum("nd,rdk->rnk", columns, gate_rows, preferred_element_type=jnp.float32)
    up_part = jnp.einsum("nd,rdk->rnk", columns, up_rows, preferred_element_type=jnp.float32)
    parts = jnp.concatenate([gate_part, up_part], axis=2).astype(jnp.bfloat16)
    parts = lax.all_to_all(parts, "rep", 0, 0, tiled=True)
    sums = jnp.sum(parts.astype(jnp.float32), axis=0)
    gate_sum, up_sum = sums[:, :hidden_width], sums[:, hidden_width:]
    units = (jax.nn.silu(gate_sum) * up_sum).astype(jnp.bfloat16)
    hidden_width = units.shape[1]
    unit_copies = jnp.broadcast_to(units[None], (rep_count,) + units.shape)
    units_all = lax.all_to_all(unit_copies, "rep", 0, 0, tiled=True)
    pieces = jnp.einsum("rnk,rkc->rnc", units_all, down_cols, preferred_element_type=jnp.float32)
    out_cols = jnp.sum(pieces.astype(jnp.bfloat16).astype(jnp.float32), axis=0)
    out_cols = out_cols.astype(jnp.bfloat16)
    out_cols = out_cols.reshape(rep_count * expert_count, capacity, chunk)
    back = lax.all_to_all(out_cols, ("rep",) + EP, 0, 0, tiled=True)
    back = back.reshape(rep_count, expert_count, capacity, chunk)
    served = jnp.transpose(back, (1, 2, 0, 3))
    mixture = jnp.dot(
        combine, served.reshape(slot_count, width).astype(jnp.float32), precision=lax.Precision.HIGHEST
    )
    return (residual + mixture)[None]


def solution(mesh):
    rep_n, ep_n = mesh.devices.shape
    fine = Mesh(mesh.devices.reshape(rep_n, ep_n // 2, 2), ("rep", "epo", "core"))
    return jax.shard_map(
        local,
        mesh=fine,
        in_specs=(
            P("rep", None, EP),
            P("rep", EP),
            P("rep", EP, None),
            P(),
            P(),
            P("rep"),
            P("rep", EP, None),
            P(EP, None, None),
            P(EP, None),
            P(),
            P("rep", EP, None),
            P("rep", EP, None),
            P(EP, None, "rep"),
            P(EP, None, "rep"),
            P(EP, "rep", None),
        ),
        out_specs=P("rep", EP, None),
        check_vma=False,
    )
```

```python
import jax
import jax.numpy as jnp
from jax import lax
from jax.sharding import Mesh, PartitionSpec as P

KVR = 512
ROPE = 64
SUF = 128
EP = ("epo", "core")


score_scale = 0.07216878364870323
norm_eps = 1e-06


def expert_units(token_rows, gate_rows, up_rows):
    gate_part = jnp.dot(token_rows, gate_rows, preferred_element_type=jnp.float32)
    up_part = jnp.dot(token_rows, up_rows, preferred_element_type=jnp.float32)
    return (jax.nn.silu(gate_part) * up_part).astype(jnp.bfloat16)


def local(
    queries,
    suffix_latent,
    cache_pool,
    holders,
    block_slots,
    prefix_len,
    hidden,
    w_value,
    w_out,
    norm_gain,
    experts,
    gate_weights,
    w_gate,
    w_up,
    w_down,
):
    rep_count = lax.axis_size("rep")
    ep_count = lax.axis_size(EP)
    rep_index = lax.axis_index("rep")
    ep_index = lax.axis_index("epo") * lax.axis_size("core") + lax.axis_index("core")
    pool_count = cache_pool.shape[1]
    block_width = cache_pool.shape[2]
    per_device = holders.shape[1] // ep_count
    per_holder = (per_device + rep_count - 1) // rep_count
    latent_width = KVR + ROPE
    mine_holders = lax.dynamic_slice_in_dim(holders, ep_index * per_device, per_device, 1)
    mine_slots = lax.dynamic_slice_in_dim(block_slots, ep_index * per_device, per_device, 1)
    position = jnp.arange(per_device, dtype=jnp.int32)
    same_holder = mine_holders[:, :, None] == mine_holders[:, None, :]
    earlier = position[None, :] < position[:, None]
    occurrence = jnp.sum((same_holder & earlier[None, :, :]).astype(jnp.int32), axis=2)
    wanted = mine_holders == rep_index
    chosen_slot = occurrence[:, :, None] == jnp.arange(per_holder, dtype=jnp.int32)[None, None, :]
    chosen_row = mine_slots[:, :, None] == jnp.arange(pool_count, dtype=jnp.int32)[None, None, :]
    selector = jnp.einsum(
        "son,soh->snh",
        (wanted[:, :, None] & chosen_slot).astype(jnp.float32),
        chosen_row.astype(jnp.float32),
        precision=lax.Precision.HIGHEST,
    )
    outgoing = jnp.dot(
        selector.reshape(rep_count * per_holder, pool_count).astype(jnp.bfloat16),
        cache_pool[0],
        preferred_element_type=jnp.float32,
    )
    outgoing = outgoing.astype(jnp.bfloat16).reshape(rep_count, per_holder, block_width)
    incoming = lax.all_to_all(outgoing, "rep", split_axis=0, concat_axis=0, tiled=True)
    own_holders = lax.dynamic_index_in_dim(mine_holders, rep_index, 0, keepdims=False)
    own_order = lax.dynamic_index_in_dim(occurrence, rep_index, 0, keepdims=False)
    source = own_holders * per_holder + own_order
    picker = (
        source[:, None] == jnp.arange(rep_count * per_holder, dtype=jnp.int32)[None, :]
    ).astype(jnp.bfloat16)
    own_blocks = jnp.dot(
        picker,
        incoming.reshape(rep_count * per_holder, block_width),
        preferred_element_type=jnp.float32,
    ).astype(jnp.bfloat16)
    core_count = lax.axis_size("core")
    outer_count = ep_count // core_count
    pre_rows = per_device * (block_width // latent_width)
    suf_rows = SUF // ep_count
    pad_rows = -(pre_rows + suf_rows) % 16
    packed = jnp.concatenate(
        [
            own_blocks.reshape(pre_rows, latent_width),
            suffix_latent.reshape(suf_rows, latent_width),
            jnp.zeros((pad_rows, latent_width), own_blocks.dtype),
        ],
        axis=0,
    )
    row_count = packed.shape[0]
    chip_keys = lax.all_gather(packed[None], EP, axis=0, tiled=True)
    hidden_width, width = w_down.shape[1], w_down.shape[2]
    chunk = width // rep_count
    down_cols = w_down[0].reshape(hidden_width, rep_count, chunk)
    down_cols = jnp.transpose(down_cols, (1, 0, 2))
    gate_rows = lax.all_to_all(w_gate[0].reshape(rep_count, chunk, hidden_width), "rep", 0, 0, tiled=True)
    up_rows = lax.all_to_all(w_up[0].reshape(rep_count, chunk, hidden_width), "rep", 0, 0, tiled=True)
    chip_keys, gate_rows, up_rows = lax.optimization_barrier((chip_keys, gate_rows, up_rows))
    keys = chip_keys.reshape(-1, latent_width)
    device_of = lax.broadcasted_iota(jnp.int32, chip_keys.shape[:2], 0).reshape(-1)
    row_of = lax.broadcasted_iota(jnp.int32, chip_keys.shape[:2], 1).reshape(-1)
    is_prefix = (row_of < pre_rows) & (device_of * pre_rows + row_of < prefix_len[0])
    suffix_pos = device_of * suf_rows + row_of - pre_rows
    is_suffix = (row_of >= pre_rows) & (row_of < pre_rows + suf_rows)
    token_pos = jnp.arange(SUF, dtype=jnp.int32)
    visible = is_prefix[None, :] | (is_suffix[None, :] & (suffix_pos[None, :] <= token_pos[:, None]))
    query_rows = queries[0].reshape(SUF, -1, latent_width)
    scores = (
        jnp.einsum("thc,kc->htk", query_rows, keys, preferred_element_type=jnp.float32)
        * score_scale
    )
    scores = jnp.where(visible[None, :, :], scores, -1e30)
    highest = jnp.max(scores, axis=2)
    exps = jnp.exp(scores - highest[:, :, None])
    denominator = jnp.sum(exps, axis=2)
    latent = jnp.einsum(
        "htk,kc->thc",
        exps.astype(jnp.bfloat16),
        keys[:, :KVR],
        preferred_element_type=jnp.float32,
    )
    latent = (latent / jnp.transpose(denominator)[:, :, None]).astype(jnp.bfloat16)
    head_values = jnp.einsum(
        "thc,hcv->thv", latent, w_value, preferred_element_type=jnp.float32
    ).astype(jnp.bfloat16)
    head_values = head_values.reshape(outer_count, core_count, suf_rows, -1)
    head_values = jnp.transpose(head_values, (1, 0, 2, 3)).reshape(SUF, -1)
    partial = jnp.dot(head_values, w_out, preferred_element_type=jnp.float32)
    partial = partial.reshape(core_count, SUF // core_count, -1)
    partial = jnp.sum(lax.all_to_all(partial, "core", 0, 0, tiled=True), axis=0)
    partial = partial.reshape(outer_count, 16, -1).astype(jnp.bfloat16)
    partial, down_cols = lax.optimization_barrier((partial, down_cols))
    down_cols = lax.all_to_all(down_cols, "rep", 0, 0, tiled=True)
    attention = jnp.sum(
        lax.all_to_all(partial, "epo", 0, 0, tiled=True).astype(jnp.float32), axis=0
    )
    attention = attention.reshape(suf_rows, -1)
    residual = hidden[0].astype(jnp.float32) + attention
    scale_rows = lax.rsqrt(jnp.mean(residual * residual, axis=1, keepdims=True) + norm_eps)
    normed = (residual * scale_rows * norm_gain.astype(jnp.float32)).astype(jnp.bfloat16)
    tok_count = hidden.shape[1]
    chosen = experts[0]
    top_count = chosen.shape[1]
    expert_count = ep_count * w_gate.shape[0]
    capacity = min(tok_count, 2 * max(1, tok_count * top_count // expert_count))
    slot_count = expert_count * capacity
    flat_choice = chosen.reshape(-1)
    hits = (flat_choice[:, None] == jnp.arange(expert_count, dtype=jnp.int32)[None, :]).astype(
        jnp.int32
    )
    rank = jnp.sum((jnp.cumsum(hits, axis=0) - hits) * hits, axis=1)
    slot_id = flat_choice * capacity + rank
    slot_hot = (slot_id[:, None] == jnp.arange(slot_count, dtype=jnp.int32)[None, :]).astype(
        jnp.float32
    )
    owner = jnp.arange(flat_choice.shape[0], dtype=jnp.int32) // top_count
    token_hot = (owner[:, None] == jnp.arange(tok_count, dtype=jnp.int32)[None, :]).astype(
        jnp.float32
    )
    placing = jnp.dot(jnp.transpose(slot_hot), token_hot, precision=lax.Precision.HIGHEST)
    weighted_hot = token_hot * gate_weights[0].astype(jnp.float32).reshape(-1)[:, None]
    combine = jnp.dot(jnp.transpose(weighted_hot), slot_hot, precision=lax.Precision.HIGHEST)
    grouped = jnp.dot(
        placing.astype(jnp.bfloat16), normed, preferred_element_type=jnp.float32
    ).astype(jnp.bfloat16)
    width = grouped.shape[1]
    spread = grouped.reshape(expert_count, capacity, rep_count, chunk)
    spread = jnp.transpose(spread, (2, 0, 1, 3)).reshape(rep_count * expert_count, capacity, chunk)
    spread, down_cols = lax.optimization_barrier((spread, down_cols))
    columns = lax.all_to_all(spread, ("rep",) + EP, 0, 0, tiled=True).reshape(-1, chunk)
    gate_part = jnp.einsum("nd,rdk->rnk", columns, gate_rows, preferred_element_type=jnp.float32)
    up_part = jnp.einsum("nd,rdk->rnk", columns, up_rows, preferred_element_type=jnp.float32)
    parts = jnp.concatenate([gate_part, up_part], axis=2).astype(jnp.bfloat16)
    parts = lax.all_to_all(parts, "rep", 0, 0, tiled=True)
    sums = jnp.sum(parts.astype(jnp.float32), axis=0)
    gate_sum, up_sum = sums[:, :hidden_width], sums[:, hidden_width:]
    units = (jax.nn.silu(gate_sum) * up_sum).astype(jnp.bfloat16)
    hidden_width = units.shape[1]
    unit_copies = jnp.broadcast_to(units[None], (rep_count,) + units.shape)
    units_all = lax.all_to_all(unit_copies, "rep", 0, 0, tiled=True)
    pieces = jnp.einsum("rnk,rkc->rnc", units_all, down_cols, preferred_element_type=jnp.float32)
    out_cols = jnp.sum(pieces.astype(jnp.bfloat16).astype(jnp.float32), axis=0)
    out_cols = out_cols.astype(jnp.bfloat16)
    out_cols = out_cols.reshape(rep_count * expert_count, capacity, chunk)
    back = lax.all_to_all(out_cols, ("rep",) + EP, 0, 0, tiled=True)
    back = back.reshape(rep_count, expert_count, capacity, chunk)
    served = jnp.transpose(back, (1, 2, 0, 3))
    mixture = jnp.dot(
        combine, served.reshape(slot_count, width).astype(jnp.float32), precision=lax.Precision.HIGHEST
    )
    return (residual + mixture)[None]


def solution(mesh):
    rep_n, ep_n = mesh.devices.shape
    fine = Mesh(mesh.devices.reshape(rep_n, ep_n // 2, 2), ("rep", "epo", "core"))
    return jax.shard_map(
        local,
        mesh=fine,
        in_specs=(
            P("rep", None, EP),
            P("rep", EP),
            P("rep", EP, None),
            P(),
            P(),
            P("rep"),
            P("rep", EP, None),
            P(EP, None, None),
            P(EP, None),
            P(),
            P("rep", EP, None),
            P("rep", EP, None),
            P(EP, None, "rep"),
            P(EP, None, "rep"),
            P(EP, "rep", None),
        ),
        out_specs=P("rep", EP, None),
        check_vma=False,
    )
```

```python
import jax
import jax.numpy as jnp
from jax import lax
from jax.sharding import Mesh, PartitionSpec as P

KVR = 512
ROPE = 64
SUF = 128
EP = ("epo", "core")


score_scale = 0.07216878364870323
norm_eps = 1e-06


def expert_units(token_rows, gate_rows, up_rows):
    gate_part = jnp.dot(token_rows, gate_rows, preferred_element_type=jnp.float32)
    up_part = jnp.dot(token_rows, up_rows, preferred_element_type=jnp.float32)
    return (jax.nn.silu(gate_part) * up_part).astype(jnp.bfloat16)


def local(
    queries,
    suffix_latent,
    cache_pool,
    holders,
    block_slots,
    prefix_len,
    hidden,
    w_value,
    w_out,
    norm_gain,
    experts,
    gate_weights,
    w_gate,
    w_up,
    w_down,
):
    rep_count = lax.axis_size("rep")
    ep_count = lax.axis_size(EP)
    rep_index = lax.axis_index("rep")
    ep_index = lax.axis_index("epo") * lax.axis_size("core") + lax.axis_index("core")
    pool_count = cache_pool.shape[1]
    block_width = cache_pool.shape[2]
    per_device = holders.shape[1] // ep_count
    per_holder = (per_device + rep_count - 1) // rep_count
    latent_width = KVR + ROPE
    mine_holders = lax.dynamic_slice_in_dim(holders, ep_index * per_device, per_device, 1)
    mine_slots = lax.dynamic_slice_in_dim(block_slots, ep_index * per_device, per_device, 1)
    position = jnp.arange(per_device, dtype=jnp.int32)
    same_holder = mine_holders[:, :, None] == mine_holders[:, None, :]
    earlier = position[None, :] < position[:, None]
    occurrence = jnp.sum((same_holder & earlier[None, :, :]).astype(jnp.int32), axis=2)
    wanted = mine_holders == rep_index
    chosen_slot = occurrence[:, :, None] == jnp.arange(per_holder, dtype=jnp.int32)[None, None, :]
    chosen_row = mine_slots[:, :, None] == jnp.arange(pool_count, dtype=jnp.int32)[None, None, :]
    selector = jnp.einsum(
        "son,soh->snh",
        (wanted[:, :, None] & chosen_slot).astype(jnp.float32),
        chosen_row.astype(jnp.float32),
        precision=lax.Precision.HIGHEST,
    )
    outgoing = jnp.dot(
        selector.reshape(rep_count * per_holder, pool_count).astype(jnp.bfloat16),
        cache_pool[0],
        preferred_element_type=jnp.float32,
    )
    outgoing = outgoing.astype(jnp.bfloat16).reshape(rep_count, per_holder, block_width)
    incoming = lax.all_to_all(outgoing, "rep", split_axis=0, concat_axis=0, tiled=True)
    own_holders = lax.dynamic_index_in_dim(mine_holders, rep_index, 0, keepdims=False)
    own_order = lax.dynamic_index_in_dim(occurrence, rep_index, 0, keepdims=False)
    source = own_holders * per_holder + own_order
    picker = (
        source[:, None] == jnp.arange(rep_count * per_holder, dtype=jnp.int32)[None, :]
    ).astype(jnp.bfloat16)
    own_blocks = jnp.dot(
        picker,
        incoming.reshape(rep_count * per_holder, block_width),
        preferred_element_type=jnp.float32,
    ).astype(jnp.bfloat16)
    core_count = lax.axis_size("core")
    outer_count = ep_count // core_count
    pre_rows = per_device * (block_width // latent_width)
    suf_rows = SUF // ep_count
    pad_rows = -(pre_rows + suf_rows) % 16
    packed = jnp.concatenate(
        [
            own_blocks.reshape(pre_rows, latent_width),
            suffix_latent.reshape(suf_rows, latent_width),
            jnp.zeros((pad_rows, latent_width), own_blocks.dtype),
        ],
        axis=0,
    )
    row_count = packed.shape[0]
    chip_keys = lax.all_gather(packed[None], EP, axis=0, tiled=True)
    hidden_width, width = w_down.shape[1], w_down.shape[2]
    chunk = width // rep_count
    down_cols = w_down[0].reshape(hidden_width, rep_count, chunk)
    down_cols = jnp.transpose(down_cols, (1, 0, 2))
    down_cols = lax.all_to_all(down_cols, "rep", 0, 0, tiled=True)
    gate_rows = lax.all_to_all(w_gate[0].reshape(rep_count, chunk, hidden_width), "rep", 0, 0, tiled=True)
    up_rows = lax.all_to_all(w_up[0].reshape(rep_count, chunk, hidden_width), "rep", 0, 0, tiled=True)
    chip_keys, down_cols, gate_rows, up_rows = lax.optimization_barrier(
        (chip_keys, down_cols, gate_rows, up_rows)
    )
    keys = chip_keys.reshape(-1, latent_width)
    device_of = lax.broadcasted_iota(jnp.int32, chip_keys.shape[:2], 0).reshape(-1)
    row_of = lax.broadcasted_iota(jnp.int32, chip_keys.shape[:2], 1).reshape(-1)
    is_prefix = (row_of < pre_rows) & (device_of * pre_rows + row_of < prefix_len[0])
    suffix_pos = device_of * suf_rows + row_of - pre_rows
    is_suffix = (row_of >= pre_rows) & (row_of < pre_rows + suf_rows)
    token_pos = jnp.arange(SUF, dtype=jnp.int32)
    visible = is_prefix[None, :] | (is_suffix[None, :] & (suffix_pos[None, :] <= token_pos[:, None]))
    query_rows = queries[0].reshape(SUF, -1, latent_width)
    scores = (
        jnp.einsum("thc,kc->htk", query_rows, keys, preferred_element_type=jnp.float32)
        * score_scale
    )
    scores = jnp.where(visible[None, :, :], scores, -1e30)
    highest = jnp.max(scores, axis=2)
    exps = jnp.exp(scores - highest[:, :, None])
    denominator = jnp.sum(exps, axis=2)
    latent = jnp.einsum(
        "htk,kc->thc",
        exps.astype(jnp.bfloat16),
        keys[:, :KVR],
        preferred_element_type=jnp.float32,
    )
    latent = (latent / jnp.transpose(denominator)[:, :, None]).astype(jnp.bfloat16)
    head_values = jnp.einsum(
        "thc,hcv->thv", latent, w_value, preferred_element_type=jnp.float32
    ).astype(jnp.bfloat16)
    head_values = head_values.reshape(outer_count, core_count, suf_rows, -1)
    head_values = jnp.transpose(head_values, (1, 0, 2, 3)).reshape(SUF, -1)
    partial = jnp.dot(head_values, w_out, preferred_element_type=jnp.float32)
    partial = partial.reshape(core_count, SUF // core_count, -1)
    partial = lax.all_to_all(partial.astype(jnp.bfloat16), "core", 0, 0, tiled=True)
    partial = jnp.sum(partial.astype(jnp.float32), axis=0)
    partial = partial.reshape(outer_count, 16, -1).astype(jnp.bfloat16)
    attention = jnp.sum(
        lax.all_to_all(partial, "epo", 0, 0, tiled=True).astype(jnp.float32), axis=0
    )
    attention = attention.reshape(suf_rows, -1)
    residual = hidden[0].astype(jnp.float32) + attention
    scale_rows = lax.rsqrt(jnp.mean(residual * residual, axis=1, keepdims=True) + norm_eps)
    normed = (residual * scale_rows * norm_gain.astype(jnp.float32)).astype(jnp.bfloat16)
    tok_count = hidden.shape[1]
    chosen = experts[0]
    top_count = chosen.shape[1]
    expert_count = ep_count * w_gate.shape[0]
    capacity = min(tok_count, 2 * max(1, tok_count * top_count // expert_count))
    slot_count = expert_count * capacity
    flat_choice = chosen.reshape(-1)
    hits = (flat_choice[:, None] == jnp.arange(expert_count, dtype=jnp.int32)[None, :]).astype(
        jnp.int32
    )
    rank = jnp.sum((jnp.cumsum(hits, axis=0) - hits) * hits, axis=1)
    slot_id = flat_choice * capacity + rank
    slot_hot = (slot_id[:, None] == jnp.arange(slot_count, dtype=jnp.int32)[None, :]).astype(
        jnp.float32
    )
    owner = jnp.arange(flat_choice.shape[0], dtype=jnp.int32) // top_count
    token_hot = (owner[:, None] == jnp.arange(tok_count, dtype=jnp.int32)[None, :]).astype(
        jnp.float32
    )
    placing = jnp.dot(jnp.transpose(slot_hot), token_hot, precision=lax.Precision.HIGHEST)
    weighted_hot = token_hot * gate_weights[0].astype(jnp.float32).reshape(-1)[:, None]
    combine = jnp.dot(jnp.transpose(weighted_hot), slot_hot, precision=lax.Precision.HIGHEST)
    grouped = jnp.dot(
        placing.astype(jnp.bfloat16), normed, preferred_element_type=jnp.float32
    ).astype(jnp.bfloat16)
    width = grouped.shape[1]
    spread = grouped.reshape(expert_count, capacity, rep_count, chunk)
    spread = jnp.transpose(spread, (2, 0, 1, 3)).reshape(rep_count * expert_count, capacity, chunk)
    columns = lax.all_to_all(spread, ("rep",) + EP, 0, 0, tiled=True).reshape(-1, chunk)
    gate_part = jnp.einsum("nd,rdk->rnk", columns, gate_rows, preferred_element_type=jnp.float32)
    up_part = jnp.einsum("nd,rdk->rnk", columns, up_rows, preferred_element_type=jnp.float32)
    parts = jnp.concatenate([gate_part, up_part], axis=2).astype(jnp.bfloat16)
    parts = lax.all_to_all(parts, "rep", 0, 0, tiled=True)
    sums = jnp.sum(parts.astype(jnp.float32), axis=0)
    gate_sum, up_sum = sums[:, :hidden_width], sums[:, hidden_width:]
    units = (jax.nn.silu(gate_sum) * up_sum).astype(jnp.bfloat16)
    hidden_width = units.shape[1]
    unit_copies = jnp.broadcast_to(units[None], (rep_count,) + units.shape)
    units_all = lax.all_to_all(unit_copies, "rep", 0, 0, tiled=True)
    pieces = jnp.einsum("rnk,rkc->rnc", units_all, down_cols, preferred_element_type=jnp.float32)
    out_cols = jnp.sum(pieces.astype(jnp.bfloat16).astype(jnp.float32), axis=0)
    out_cols = out_cols.astype(jnp.bfloat16)
    out_cols = out_cols.reshape(rep_count * expert_count, capacity, chunk)
    back = lax.all_to_all(out_cols, ("rep",) + EP, 0, 0, tiled=True)
    back = back.reshape(rep_count, expert_count, capacity, chunk)
    served = jnp.transpose(back, (1, 2, 0, 3))
    mixture = jnp.dot(
        combine, served.reshape(slot_count, width).astype(jnp.float32), precision=lax.Precision.HIGHEST
    )
    return (residual + mixture)[None]


def solution(mesh):
    rep_n, ep_n = mesh.devices.shape
    fine = Mesh(mesh.devices.reshape(rep_n, ep_n // 2, 2), ("rep", "epo", "core"))
    return jax.shard_map(
        local,
        mesh=fine,
        in_specs=(
            P("rep", None, EP),
            P("rep", EP),
            P("rep", EP, None),
            P(),
            P(),
            P("rep"),
            P("rep", EP, None),
            P(EP, None, None),
            P(EP, None),
            P(),
            P("rep", EP, None),
            P("rep", EP, None),
            P(EP, None, "rep"),
            P(EP, None, "rep"),
            P(EP, "rep", None),
        ),
        out_specs=P("rep", EP, None),
        check_vma=False,
    )
```

```python
import jax
import jax.numpy as jnp
from jax import lax
from jax.sharding import Mesh, PartitionSpec as P

KVR = 512
ROPE = 64
SUF = 128
EP = ("epo", "core")


score_scale = 0.07216878364870323
norm_eps = 1e-06


def expert_units(token_rows, gate_rows, up_rows):
    gate_part = jnp.dot(token_rows, gate_rows, preferred_element_type=jnp.float32)
    up_part = jnp.dot(token_rows, up_rows, preferred_element_type=jnp.float32)
    return (jax.nn.silu(gate_part) * up_part).astype(jnp.bfloat16)


def local(
    queries,
    suffix_latent,
    cache_pool,
    holders,
    block_slots,
    prefix_len,
    hidden,
    w_value,
    w_out,
    norm_gain,
    experts,
    gate_weights,
    w_gate,
    w_up,
    w_down,
):
    rep_count = lax.axis_size("rep")
    ep_count = lax.axis_size(EP)
    rep_index = lax.axis_index("rep")
    ep_index = lax.axis_index("epo") * lax.axis_size("core") + lax.axis_index("core")
    pool_count = cache_pool.shape[1]
    block_width = cache_pool.shape[2]
    per_device = holders.shape[1] // ep_count
    per_holder = (per_device + rep_count - 1) // rep_count
    latent_width = KVR + ROPE
    mine_holders = lax.dynamic_slice_in_dim(holders, ep_index * per_device, per_device, 1)
    mine_slots = lax.dynamic_slice_in_dim(block_slots, ep_index * per_device, per_device, 1)
    position = jnp.arange(per_device, dtype=jnp.int32)
    same_holder = mine_holders[:, :, None] == mine_holders[:, None, :]
    earlier = position[None, :] < position[:, None]
    occurrence = jnp.sum((same_holder & earlier[None, :, :]).astype(jnp.int32), axis=2)
    wanted = mine_holders == rep_index
    chosen_slot = occurrence[:, :, None] == jnp.arange(per_holder, dtype=jnp.int32)[None, None, :]
    chosen_row = mine_slots[:, :, None] == jnp.arange(pool_count, dtype=jnp.int32)[None, None, :]
    selector = jnp.einsum(
        "son,soh->snh",
        (wanted[:, :, None] & chosen_slot).astype(jnp.float32),
        chosen_row.astype(jnp.float32),
        precision=lax.Precision.HIGHEST,
    )
    outgoing = jnp.dot(
        selector.reshape(rep_count * per_holder, pool_count).astype(jnp.bfloat16),
        cache_pool[0],
        preferred_element_type=jnp.float32,
    )
    outgoing = outgoing.astype(jnp.bfloat16).reshape(rep_count, per_holder, block_width)
    incoming = lax.all_to_all(outgoing, "rep", split_axis=0, concat_axis=0, tiled=True)
    own_holders = lax.dynamic_index_in_dim(mine_holders, rep_index, 0, keepdims=False)
    own_order = lax.dynamic_index_in_dim(occurrence, rep_index, 0, keepdims=False)
    source = own_holders * per_holder + own_order
    picker = (
        source[:, None] == jnp.arange(rep_count * per_holder, dtype=jnp.int32)[None, :]
    ).astype(jnp.bfloat16)
    own_blocks = jnp.dot(
        picker,
        incoming.reshape(rep_count * per_holder, block_width),
        preferred_element_type=jnp.float32,
    ).astype(jnp.bfloat16)
    core_count = lax.axis_size("core")
    outer_count = ep_count // core_count
    pre_rows = per_device * (block_width // latent_width)
    suf_rows = SUF // ep_count
    pad_rows = -(pre_rows + suf_rows) % 16
    packed = jnp.concatenate(
        [
            own_blocks.reshape(pre_rows, latent_width),
            suffix_latent.reshape(suf_rows, latent_width),
            jnp.zeros((pad_rows, latent_width), own_blocks.dtype),
        ],
        axis=0,
    )
    row_count = packed.shape[0]
    chip_keys = lax.all_gather(packed[None], EP, axis=0, tiled=True)
    hidden_width, width = w_down.shape[1], w_down.shape[2]
    chunk = width // rep_count
    down_cols = w_down[0].reshape(hidden_width, rep_count, chunk)
    down_cols = jnp.transpose(down_cols, (1, 0, 2))
    down_cols = lax.all_to_all(down_cols, "rep", 0, 0, tiled=True)
    gate_up = jnp.concatenate(
        [
            w_gate[0].reshape(rep_count, chunk, hidden_width),
            w_up[0].reshape(rep_count, chunk, hidden_width),
        ],
        axis=2,
    )
    gate_up = lax.all_to_all(gate_up, "rep", 0, 0, tiled=True)
    chip_keys, down_cols, gate_up = lax.optimization_barrier((chip_keys, down_cols, gate_up))
    keys = chip_keys.reshape(-1, latent_width)
    device_of = lax.broadcasted_iota(jnp.int32, chip_keys.shape[:2], 0).reshape(-1)
    row_of = lax.broadcasted_iota(jnp.int32, chip_keys.shape[:2], 1).reshape(-1)
    is_prefix = (row_of < pre_rows) & (device_of * pre_rows + row_of < prefix_len[0])
    suffix_pos = device_of * suf_rows + row_of - pre_rows
    is_suffix = (row_of >= pre_rows) & (row_of < pre_rows + suf_rows)
    token_pos = jnp.arange(SUF, dtype=jnp.int32)
    visible = is_prefix[None, :] | (is_suffix[None, :] & (suffix_pos[None, :] <= token_pos[:, None]))
    query_rows = queries[0].reshape(SUF, -1, latent_width)
    scores = (
        jnp.einsum("thc,kc->htk", query_rows, keys, preferred_element_type=jnp.float32)
        * score_scale
    )
    scores = jnp.where(visible[None, :, :], scores, -1e30)
    highest = jnp.max(scores, axis=2)
    exps = jnp.exp(scores - highest[:, :, None])
    denominator = jnp.sum(exps, axis=2)
    latent = jnp.einsum(
        "htk,kc->thc",
        exps.astype(jnp.bfloat16),
        keys[:, :KVR],
        preferred_element_type=jnp.float32,
    )
    latent = (latent / jnp.transpose(denominator)[:, :, None]).astype(jnp.bfloat16)
    head_values = jnp.einsum(
        "thc,hcv->thv", latent, w_value, preferred_element_type=jnp.float32
    ).astype(jnp.bfloat16)
    head_values = head_values.reshape(outer_count, core_count, suf_rows, -1)
    head_values = jnp.transpose(head_values, (1, 0, 2, 3)).reshape(SUF, -1)
    partial = jnp.dot(head_values, w_out, preferred_element_type=jnp.float32)
    partial = partial.reshape(core_count, SUF // core_count, -1)
    partial = lax.all_to_all(partial.astype(jnp.bfloat16), "core", 0, 0, tiled=True)
    partial = jnp.sum(partial.astype(jnp.float32), axis=0)
    partial = partial.reshape(outer_count, 16, -1).astype(jnp.bfloat16)
    attention = jnp.sum(
        lax.all_to_all(partial, "epo", 0, 0, tiled=True).astype(jnp.float32), axis=0
    )
    attention = attention.reshape(suf_rows, -1)
    residual = hidden[0].astype(jnp.float32) + attention
    scale_rows = lax.rsqrt(jnp.mean(residual * residual, axis=1, keepdims=True) + norm_eps)
    normed = (residual * scale_rows * norm_gain.astype(jnp.float32)).astype(jnp.bfloat16)
    tok_count = hidden.shape[1]
    chosen = experts[0]
    top_count = chosen.shape[1]
    expert_count = ep_count * w_gate.shape[0]
    capacity = min(tok_count, 2 * max(1, tok_count * top_count // expert_count))
    slot_count = expert_count * capacity
    flat_choice = chosen.reshape(-1)
    hits = (flat_choice[:, None] == jnp.arange(expert_count, dtype=jnp.int32)[None, :]).astype(
        jnp.int32
    )
    rank = jnp.sum((jnp.cumsum(hits, axis=0) - hits) * hits, axis=1)
    slot_id = flat_choice * capacity + rank
    slot_hot = (slot_id[:, None] == jnp.arange(slot_count, dtype=jnp.int32)[None, :]).astype(
        jnp.float32
    )
    owner = jnp.arange(flat_choice.shape[0], dtype=jnp.int32) // top_count
    token_hot = (owner[:, None] == jnp.arange(tok_count, dtype=jnp.int32)[None, :]).astype(
        jnp.float32
    )
    placing = jnp.dot(jnp.transpose(slot_hot), token_hot, precision=lax.Precision.HIGHEST)
    weighted_hot = token_hot * gate_weights[0].astype(jnp.float32).reshape(-1)[:, None]
    combine = jnp.dot(jnp.transpose(weighted_hot), slot_hot, precision=lax.Precision.HIGHEST)
    grouped = jnp.dot(
        placing.astype(jnp.bfloat16), normed, preferred_element_type=jnp.float32
    ).astype(jnp.bfloat16)
    width = grouped.shape[1]
    spread = grouped.reshape(expert_count, capacity, rep_count, chunk)
    spread = jnp.transpose(spread, (2, 0, 1, 3)).reshape(rep_count * expert_count, capacity, chunk)
    columns = lax.all_to_all(spread, ("rep",) + EP, 0, 0, tiled=True).reshape(-1, chunk)
    parts = jnp.einsum("nd,rdk->rnk", columns, gate_up, preferred_element_type=jnp.float32)
    parts = parts.astype(jnp.bfloat16)
    parts = lax.all_to_all(parts, "rep", 0, 0, tiled=True)
    sums = jnp.sum(parts.astype(jnp.float32), axis=0)
    gate_sum, up_sum = sums[:, :hidden_width], sums[:, hidden_width:]
    units = (jax.nn.silu(gate_sum) * up_sum).astype(jnp.bfloat16)
    hidden_width = units.shape[1]
    unit_copies = jnp.broadcast_to(units[None], (rep_count,) + units.shape)
    units_all = lax.all_to_all(unit_copies, "rep", 0, 0, tiled=True)
    pieces = jnp.einsum("rnk,rkc->rnc", units_all, down_cols, preferred_element_type=jnp.float32)
    out_cols = jnp.sum(pieces.astype(jnp.bfloat16).astype(jnp.float32), axis=0)
    out_cols = out_cols.astype(jnp.bfloat16)
    out_cols = out_cols.reshape(rep_count * expert_count, capacity, chunk)
    back = lax.all_to_all(out_cols, ("rep",) + EP, 0, 0, tiled=True)
    back = back.reshape(rep_count, expert_count, capacity, chunk)
    served = jnp.transpose(back, (1, 2, 0, 3))
    mixture = jnp.dot(
        combine, served.reshape(slot_count, width).astype(jnp.float32), precision=lax.Precision.HIGHEST
    )
    return (residual + mixture)[None]


def solution(mesh):
    rep_n, ep_n = mesh.devices.shape
    fine = Mesh(mesh.devices.reshape(rep_n, ep_n // 2, 2), ("rep", "epo", "core"))
    return jax.shard_map(
        local,
        mesh=fine,
        in_specs=(
            P("rep", None, EP),
            P("rep", EP),
            P("rep", EP, None),
            P(),
            P(),
            P("rep"),
            P("rep", EP, None),
            P(EP, None, None),
            P(EP, None),
            P(),
            P("rep", EP, None),
            P("rep", EP, None),
            P(EP, None, "rep"),
            P(EP, None, "rep"),
            P(EP, "rep", None),
        ),
        out_specs=P("rep", EP, None),
        check_vma=False,
    )
```

```python
import jax
import jax.numpy as jnp
from jax import lax
from jax.sharding import Mesh, PartitionSpec as P

KVR = 512
ROPE = 64
SUF = 128
EP = ("epo", "core")


score_scale = 0.07216878364870323
norm_eps = 1e-06


def expert_units(token_rows, gate_rows, up_rows):
    gate_part = jnp.dot(token_rows, gate_rows, preferred_element_type=jnp.float32)
    up_part = jnp.dot(token_rows, up_rows, preferred_element_type=jnp.float32)
    return (jax.nn.silu(gate_part) * up_part).astype(jnp.bfloat16)


def local(
    queries,
    suffix_latent,
    cache_pool,
    holders,
    block_slots,
    prefix_len,
    hidden,
    w_value,
    w_out,
    norm_gain,
    experts,
    gate_weights,
    w_gate,
    w_up,
    w_down,
):
    rep_count = lax.axis_size("rep")
    ep_count = lax.axis_size(EP)
    rep_index = lax.axis_index("rep")
    ep_index = lax.axis_index("epo") * lax.axis_size("core") + lax.axis_index("core")
    pool_count = cache_pool.shape[1]
    block_width = cache_pool.shape[2]
    per_device = holders.shape[1] // ep_count
    per_holder = (per_device + rep_count - 1) // rep_count
    latent_width = KVR + ROPE
    mine_holders = lax.dynamic_slice_in_dim(holders, ep_index * per_device, per_device, 1)
    mine_slots = lax.dynamic_slice_in_dim(block_slots, ep_index * per_device, per_device, 1)
    position = jnp.arange(per_device, dtype=jnp.int32)
    same_holder = mine_holders[:, :, None] == mine_holders[:, None, :]
    earlier = position[None, :] < position[:, None]
    occurrence = jnp.sum((same_holder & earlier[None, :, :]).astype(jnp.int32), axis=2)
    wanted = mine_holders == rep_index
    chosen_slot = occurrence[:, :, None] == jnp.arange(per_holder, dtype=jnp.int32)[None, None, :]
    chosen_row = mine_slots[:, :, None] == jnp.arange(pool_count, dtype=jnp.int32)[None, None, :]
    selector = jnp.einsum(
        "son,soh->snh",
        (wanted[:, :, None] & chosen_slot).astype(jnp.float32),
        chosen_row.astype(jnp.float32),
        precision=lax.Precision.HIGHEST,
    )
    outgoing = jnp.dot(
        selector.reshape(rep_count * per_holder, pool_count).astype(jnp.bfloat16),
        cache_pool[0],
        preferred_element_type=jnp.float32,
    )
    outgoing = outgoing.astype(jnp.bfloat16).reshape(rep_count, per_holder, block_width)
    hidden_width, width = w_down.shape[1], w_down.shape[2]
    chunk = width // rep_count
    down_cols = w_down[0].reshape(hidden_width, rep_count, chunk)
    down_cols = jnp.transpose(down_cols, (1, 0, 2))
    down_cols = lax.all_to_all(down_cols, "rep", 0, 0, tiled=True)
    outgoing, down_cols = lax.optimization_barrier((outgoing, down_cols))
    incoming = lax.all_to_all(outgoing, "rep", split_axis=0, concat_axis=0, tiled=True)
    own_holders = lax.dynamic_index_in_dim(mine_holders, rep_index, 0, keepdims=False)
    own_order = lax.dynamic_index_in_dim(occurrence, rep_index, 0, keepdims=False)
    source = own_holders * per_holder + own_order
    picker = (
        source[:, None] == jnp.arange(rep_count * per_holder, dtype=jnp.int32)[None, :]
    ).astype(jnp.bfloat16)
    own_blocks = jnp.dot(
        picker,
        incoming.reshape(rep_count * per_holder, block_width),
        preferred_element_type=jnp.float32,
    ).astype(jnp.bfloat16)
    core_count = lax.axis_size("core")
    outer_count = ep_count // core_count
    pre_rows = per_device * (block_width // latent_width)
    suf_rows = SUF // ep_count
    pad_rows = -(pre_rows + suf_rows) % 16
    packed = jnp.concatenate(
        [
            own_blocks.reshape(pre_rows, latent_width),
            suffix_latent.reshape(suf_rows, latent_width),
            jnp.zeros((pad_rows, latent_width), own_blocks.dtype),
        ],
        axis=0,
    )
    row_count = packed.shape[0]
    chip_keys = lax.all_gather(packed[None], EP, axis=0, tiled=True)
    gate_rows = lax.all_to_all(w_gate[0].reshape(rep_count, chunk, hidden_width), "rep", 0, 0, tiled=True)
    up_rows = lax.all_to_all(w_up[0].reshape(rep_count, chunk, hidden_width), "rep", 0, 0, tiled=True)
    chip_keys, gate_rows, up_rows = lax.optimization_barrier((chip_keys, gate_rows, up_rows))
    keys = chip_keys.reshape(-1, latent_width)
    device_of = lax.broadcasted_iota(jnp.int32, chip_keys.shape[:2], 0).reshape(-1)
    row_of = lax.broadcasted_iota(jnp.int32, chip_keys.shape[:2], 1).reshape(-1)
    is_prefix = (row_of < pre_rows) & (device_of * pre_rows + row_of < prefix_len[0])
    suffix_pos = device_of * suf_rows + row_of - pre_rows
    is_suffix = (row_of >= pre_rows) & (row_of < pre_rows + suf_rows)
    token_pos = jnp.arange(SUF, dtype=jnp.int32)
    visible = is_prefix[None, :] | (is_suffix[None, :] & (suffix_pos[None, :] <= token_pos[:, None]))
    query_rows = queries[0].reshape(SUF, -1, latent_width)
    scores = (
        jnp.einsum("thc,kc->htk", query_rows, keys, preferred_element_type=jnp.float32)
        * score_scale
    )
    scores = jnp.where(visible[None, :, :], scores, -1e30)
    highest = jnp.max(scores, axis=2)
    exps = jnp.exp(scores - highest[:, :, None])
    denominator = jnp.sum(exps, axis=2)
    latent = jnp.einsum(
        "htk,kc->thc",
        exps.astype(jnp.bfloat16),
        keys[:, :KVR],
        preferred_element_type=jnp.float32,
    )
    latent = (latent / jnp.transpose(denominator)[:, :, None]).astype(jnp.bfloat16)
    head_values = jnp.einsum(
        "thc,hcv->thv", latent, w_value, preferred_element_type=jnp.float32
    ).astype(jnp.bfloat16)
    head_values = head_values.reshape(outer_count, core_count, suf_rows, -1)
    head_values = jnp.transpose(head_values, (1, 0, 2, 3)).reshape(SUF, -1)
    partial = jnp.dot(head_values, w_out, preferred_element_type=jnp.float32)
    partial = partial.reshape(core_count, SUF // core_count, -1)
    partial = lax.all_to_all(partial.astype(jnp.bfloat16), "core", 0, 0, tiled=True)
    partial = jnp.sum(partial.astype(jnp.float32), axis=0)
    partial = partial.reshape(outer_count, 16, -1).astype(jnp.bfloat16)
    attention = jnp.sum(
        lax.all_to_all(partial, "epo", 0, 0, tiled=True).astype(jnp.float32), axis=0
    )
    attention = attention.reshape(suf_rows, -1)
    residual = hidden[0].astype(jnp.float32) + attention
    scale_rows = lax.rsqrt(jnp.mean(residual * residual, axis=1, keepdims=True) + norm_eps)
    normed = (residual * scale_rows * norm_gain.astype(jnp.float32)).astype(jnp.bfloat16)
    tok_count = hidden.shape[1]
    chosen = experts[0]
    top_count = chosen.shape[1]
    expert_count = ep_count * w_gate.shape[0]
    capacity = min(tok_count, 2 * max(1, tok_count * top_count // expert_count))
    slot_count = expert_count * capacity
    flat_choice = chosen.reshape(-1)
    hits = (flat_choice[:, None] == jnp.arange(expert_count, dtype=jnp.int32)[None, :]).astype(
        jnp.int32
    )
    rank = jnp.sum((jnp.cumsum(hits, axis=0) - hits) * hits, axis=1)
    slot_id = flat_choice * capacity + rank
    slot_hot = (slot_id[:, None] == jnp.arange(slot_count, dtype=jnp.int32)[None, :]).astype(
        jnp.float32
    )
    owner = jnp.arange(flat_choice.shape[0], dtype=jnp.int32) // top_count
    token_hot = (owner[:, None] == jnp.arange(tok_count, dtype=jnp.int32)[None, :]).astype(
        jnp.float32
    )
    placing = jnp.dot(jnp.transpose(slot_hot), token_hot, precision=lax.Precision.HIGHEST)
    weighted_hot = token_hot * gate_weights[0].astype(jnp.float32).reshape(-1)[:, None]
    combine = jnp.dot(jnp.transpose(weighted_hot), slot_hot, precision=lax.Precision.HIGHEST)
    grouped = jnp.dot(
        placing.astype(jnp.bfloat16), normed, preferred_element_type=jnp.float32
    ).astype(jnp.bfloat16)
    width = grouped.shape[1]
    spread = grouped.reshape(expert_count, capacity, rep_count, chunk)
    spread = jnp.transpose(spread, (2, 0, 1, 3)).reshape(rep_count * expert_count, capacity, chunk)
    columns = lax.all_to_all(spread, ("rep",) + EP, 0, 0, tiled=True).reshape(-1, chunk)
    gate_part = jnp.einsum("nd,rdk->rnk", columns, gate_rows, preferred_element_type=jnp.float32)
    up_part = jnp.einsum("nd,rdk->rnk", columns, up_rows, preferred_element_type=jnp.float32)
    parts = jnp.concatenate([gate_part, up_part], axis=2).astype(jnp.bfloat16)
    parts = lax.all_to_all(parts, "rep", 0, 0, tiled=True)
    sums = jnp.sum(parts.astype(jnp.float32), axis=0)
    gate_sum, up_sum = sums[:, :hidden_width], sums[:, hidden_width:]
    units = (jax.nn.silu(gate_sum) * up_sum).astype(jnp.bfloat16)
    hidden_width = units.shape[1]
    unit_copies = jnp.broadcast_to(units[None], (rep_count,) + units.shape)
    units_all = lax.all_to_all(unit_copies, "rep", 0, 0, tiled=True)
    pieces = jnp.einsum("rnk,rkc->rnc", units_all, down_cols, preferred_element_type=jnp.float32)
    out_cols = jnp.sum(pieces.astype(jnp.bfloat16).astype(jnp.float32), axis=0)
    out_cols = out_cols.astype(jnp.bfloat16)
    out_cols = out_cols.reshape(rep_count * expert_count, capacity, chunk)
    back = lax.all_to_all(out_cols, ("rep",) + EP, 0, 0, tiled=True)
    back = back.reshape(rep_count, expert_count, capacity, chunk)
    served = jnp.transpose(back, (1, 2, 0, 3))
    mixture = jnp.dot(
        combine, served.reshape(slot_count, width).astype(jnp.float32), precision=lax.Precision.HIGHEST
    )
    return (residual + mixture)[None]


def solution(mesh):
    rep_n, ep_n = mesh.devices.shape
    fine = Mesh(mesh.devices.reshape(rep_n, ep_n // 2, 2), ("rep", "epo", "core"))
    return jax.shard_map(
        local,
        mesh=fine,
        in_specs=(
            P("rep", None, EP),
            P("rep", EP),
            P("rep", EP, None),
            P(),
            P(),
            P("rep"),
            P("rep", EP, None),
            P(EP, None, None),
            P(EP, None),
            P(),
            P("rep", EP, None),
            P("rep", EP, None),
            P(EP, None, "rep"),
            P(EP, None, "rep"),
            P(EP, "rep", None),
        ),
        out_specs=P("rep", EP, None),
        check_vma=False,
    )
```
